128 devices in a mesh: tok: 16 (over y, x), head: 8 (over z, core).
Axes of the slice: x: 4, y: 4, z: 4, core: 2. Of those that a mesh axis runs over, the one named last changes fastest.
Arguments:
- tokens: bfloat16 [8192, 8192], P('tok', 'head'), may hold values from -60 to 60
- gain: bfloat16 [8192], P('head'), may hold values from 0.5 to 2
- w_query: bfloat16 [8192, 8, 512], P(('head', 'tok')), may hold values from -0.125 to 0.125
- w_key: bfloat16 [8192, 8, 128], P(('head', 'tok')), may hold values from -0.0625 to 0.0625
- w_value: bfloat16 [8192, 8, 128], P(('head', 'tok')), may hold values from -0.5 to 0.5
- group_ids: int32 [8192, 1], P('tok'), may hold values from 0 to 15; in each aligned block of 512 rows (0 to 511, 512 to 1023, ...) at most 64 rows name the same one
- key_pages: bfloat16 [1024, 128, 8, 128], P('tok', None, 'head'), may hold values from -42 to 42
- value_pages: bfloat16 [1024, 128, 8, 128], P('tok', None, 'head'), may hold values from -48 to 48
- page_table: int32 [16, 32], P('tok'), may hold values from 0 to 1023, as said below
Outputs:
- attention: bfloat16 [8192, 4096], P('tok', 'head')
The draws below stay inside these ranges and needn't reach their ends.
Inputs may be any that keep to these rules, and one draw needn't show every extreme that they name: `group_ids`: among the 512 tokens of one index of tok (aligned blocks of rows), no group appears more than 64 times, a bound that some block reaches. `page_table`: row g lists 32 different pages, all in g * 64 to (g + 1) * 64 - 1, among them the first and the last page of that range.
All inputs are finite; a program needn't handle non-finite values.
Results may differ from the reference program's by a relative error of at most 0.0085.
The reference program's roundings to bfloat16 on the way count: a program that leaves them out, or rounds other values in their place, can miss the bound.
Values may be sent and summed in bfloat16 or wider, within the bound.
No kernel may reach another device: no remote copies, remote signals or barrier semaphores. Data moves between devices by JAX's collectives and lax.ppermute only.
A program may use at most 128 MiB of HBM per device.

```python
import math
import jax
import jax.numpy as jnp
import numpy as np
from jax import lax

D = 8192
HD = 128
GQ = 4
ROW_TOK = 512
PAGE = 128
PAGES_GRP = 32
POOL_DEV = 64
KV = 8
GROUPS = 16
CAP = 64
TOKENS = 8192
PAGES = 1024
PREFIX = 4096
N_TOK = 16


def draw_tokens(key, part):
    base_key = jax.random.fold_in(key, 3)
    first_key, second_key, third_key = jax.random.split(base_key, 3)
    ramp = 3.0 ** (jnp.arange(D, dtype=jnp.float32) / max(D - 1, 1))
    spread = 10.0 ** jax.random.uniform(second_key, (D,), jnp.float32)
    row_scale = 10.0 ** jax.random.uniform(third_key, (TOKENS, 1), jnp.float32)
    base = jnp.clip(jax.random.normal(first_key, (TOKENS, D), jnp.float32), -4.0, 4.0)
    return (0.05 * base * ramp[None, :] * spread[None, :] * row_scale).astype(jnp.bfloat16)


def draw_key_pages(key, part):
    base_key = jax.random.fold_in(key, 5)
    first_key = jax.random.fold_in(base_key, 0)
    shape = (PAGES, PAGE, KV, HD)
    values = jnp.clip(jax.random.normal(first_key, shape, jnp.float32), -4.0, 4.0)
    return values.astype(jnp.bfloat16)


def draw_page_table(key, part):
    base_key = jax.random.fold_in(key, 11)
    group_keys = jax.random.split(base_key, GROUPS)

    def shuffle_pool(group_key):
        middle_key, order_key = jax.random.split(group_key)
        middle = jax.random.permutation(middle_key, POOL_DEV - 2).astype(jnp.int32) + 1
        ends = jnp.array([0, POOL_DEV - 1], dtype=jnp.int32)
        chosen = jnp.concatenate([ends, middle[:PAGES_GRP - 2]])
        arrangement = jax.random.permutation(order_key, PAGES_GRP)
        return chosen[arrangement].astype(jnp.int32)
    picks = jax.vmap(shuffle_pool)(group_keys)
    offsets = POOL_DEV * jnp.arange(GROUPS, dtype=jnp.int32)[:, None]
    return (picks + offsets).astype(jnp.int32)


def level_of(own_key, shape, pieces, least, largest):
    def one(axis_at, parts):
        heights = jax.random.uniform(jax.random.fold_in(jax.random.fold_in(own_key, 6), axis_at), (parts,), jnp.float32, least / len(pieces), largest / len(pieces))
        return jnp.repeat(jnp.exp(heights), shape[axis_at] // parts).reshape((-1,) + (1,) * (len(shape) - axis_at - 1))

    loudness = one(*pieces[0])
    for cut in pieces[1:]:
        loudness = loudness * one(*cut)
    return loudness


def assign_block(stream_key, own, number, rows, number_of, top, reach, slope):
    order = jax.random.permutation(stream_key, number_of)
    heavy_load, usual = portions_of(number_of, rows * top, reach, slope, True), portions_of(number_of, rows * top, reach, slope, False)
    places = jnp.arange(number_of)

    def named(sizes, turn):
        used = int((sizes > 0).sum())
        fixed = max(1, used // 4)
        moved = fixed + (places - fixed + turn * (used - fixed)) % max(1, number_of - fixed)
        return jnp.zeros((number_of,), jnp.int32).at[order[jnp.where(places < fixed, places, moved)]].set(jnp.asarray(sizes, jnp.int32))

    sizes = jnp.where(number % 4 == 0, named(heavy_load, number // 4), named(usual, number - number // 4 - 1))
    mixed = jax.random.permutation(jax.random.fold_in(own, 3), number_of)
    donor, receiver = mixed[0:number_of // 2 * 2:2], mixed[1:number_of // 2 * 2:2]
    margin = jnp.minimum(sizes[donor] - 1, reach - sizes[receiver]) // 2
    margin = jnp.where((donor == order[0]) | (receiver == order[0]) | (sizes[receiver] == 0), 0, jnp.maximum(margin, 0))
    moved = jax.random.randint(jax.random.fold_in(own, 4), (number_of // 2,), 0, 1 << 20) % (margin + 1)
    sizes = sizes.at[donor].add(-moved).at[receiver].add(moved)
    labels = jnp.searchsorted(jnp.cumsum(sizes), jnp.arange(rows * top), side="right").astype(jnp.int32)
    listing = labels.reshape(top, rows).T
    listing = listing[jax.random.permutation(jax.random.fold_in(own, 1), rows)]
    turn = jax.random.randint(jax.random.fold_in(own, 2), (rows, 1), 0, top)
    return jnp.take_along_axis(listing, (jnp.arange(top)[None, :] + turn) % top, axis=1)


def portions_of(number_of, total, limit, slope, full):
    loads = [(1 << 20) // math.isqrt(rank ** slope) + 1 for rank in range(1, number_of + 1)]
    largest = limit if full else min(limit, max(-(-total // number_of), total * loads[0] // sum(loads)))
    least = 1 if total - largest >= number_of - 1 else 0
    holding, spare = [largest] + [least] * (number_of - 1), total - largest - least * (number_of - 1)
    while spare > 0:
        free = [i for i in range(1, number_of) if holding[i] < largest] or [i for i in range(1, number_of) if holding[i] < limit]
        pool, budget = sum([loads[i] for i in free]), spare
        for i in free:
            addition = min(limit - holding[i], max(1, budget * loads[i] // pool), spare)
            holding[i] = holding[i] + addition
            spare = spare - addition
    return np.array(holding)


def bell_draw(rng, extent, deviation, bound, cuts=(), held_as=jnp.bfloat16):
    values = deviation * jax.random.normal(rng, extent, jnp.float32)
    if cuts:
        values = values * level_of(rng, extent, cuts, -0.22, 0.18)
    return jnp.clip(values, -bound, bound).astype(held_as)


def setup_inputs(seed: int = 0) -> dict:
    keys = jax.random.split(jax.random.key(seed), 10)
    tokens = draw_tokens(jax.random.fold_in(keys[9], 71), 0)
    gain = jnp.clip(jnp.exp(math.log(2.0) - 1.3862944 * jax.random.uniform(keys[1], (D,), jnp.float32) ** level_of(keys[1], (D,), ((0, 8),), -0.2, 0.2)), 0.5, 2.0).astype(jnp.bfloat16)
    w_query = bell_draw(keys[2], (D, KV, GQ * HD), (D // 4) ** -0.5, 0.125, ((0, 128),))
    w_key = bell_draw(keys[3], (D, KV, HD), D ** -0.5, 0.0625, ((0, 128),))
    w_value = bell_draw(keys[4], (D, KV, HD), (D // 64) ** -0.5, 0.5, ((0, 128),))
    group_ids_keys = jax.random.split(jax.random.fold_in(keys[5], 1), TOKENS // ROW_TOK)
    group_ids_turns = jax.random.permutation(jax.random.fold_in(keys[5], 3), TOKENS // ROW_TOK)
    group_ids = jax.vmap(lambda own, number: assign_block(jax.random.fold_in(keys[5], 2), own, number, ROW_TOK, GROUPS, 1, CAP, 1))(group_ids_keys, group_ids_turns).reshape((TOKENS, 1))
    key_pages = draw_key_pages(jax.random.fold_in(keys[9], 71), 0)
    value_pages = bell_draw(keys[7], (PAGES, PAGE, KV, HD), 8.0, 48.0, ((0, 16), (2, 8)))
    page_table = draw_page_table(jax.random.fold_in(keys[9], 71), 0)
    return dict(tokens=tokens, gain=gain, w_query=w_query, w_key=w_key, w_value=w_value, group_ids=group_ids, key_pages=key_pages, value_pages=value_pages, page_table=page_table)


EPS = 1e-05
THETA = 10000.0

def rotate(values, positions):
    halfway = values.shape[-1] // 2
    frequency = jnp.exp(-math.log(THETA) * 2.0 * jnp.arange(halfway, dtype=jnp.float32) / values.shape[-1])
    angles = positions.astype(jnp.float32)[:, None] * frequency[None, :]
    cosine = jnp.cos(angles)[:, None, :]
    sine_part = jnp.sin(angles)[:, None, :]
    leading = values[..., :halfway].astype(jnp.float32)
    trailing = values[..., halfway:].astype(jnp.float32)
    return jnp.concatenate([leading * cosine - trailing * sine_part, trailing * cosine + leading * sine_part], axis=-1).astype(jnp.bfloat16)

def attend(queries, query_rank, prefix_keys, prefix_values, new_keys, new_values, key_rank, key_live):
    scaling = 1.0 / math.sqrt(queries.shape[-1])
    query_wide = queries.astype(jnp.float32)
    before = jnp.einsum('bhd,pd->bhp', query_wide, prefix_keys.astype(jnp.float32)) * scaling
    inside = jnp.einsum('bhd,sd->bhs', query_wide, new_keys.astype(jnp.float32)) * scaling
    allowed = key_live[None, :] & (key_rank[None, :] <= query_rank[:, None])
    inside = jnp.where(allowed[:, None, :], inside, -jnp.inf)
    highest = jnp.maximum(lax.optimization_barrier(jnp.max(before, axis=-1)), lax.optimization_barrier(jnp.max(inside, axis=-1)))
    expo_before = jnp.exp(before - highest[..., None])
    expo_inside = jnp.exp(inside - highest[..., None])
    totals = lax.optimization_barrier(jnp.sum(expo_before, axis=-1)) + lax.optimization_barrier(jnp.sum(expo_inside, axis=-1))
    probs_before = lax.optimization_barrier(expo_before.astype(jnp.bfloat16)).astype(jnp.float32)
    probs_inside = lax.optimization_barrier(expo_inside.astype(jnp.bfloat16)).astype(jnp.float32)
    mixed = jnp.einsum('bhp,pd->bhd', probs_before, prefix_values.astype(jnp.float32))
    mixed = mixed + jnp.einsum('bhs,sd->bhd', probs_inside, new_values.astype(jnp.float32))
    return (mixed / totals[..., None]).astype(jnp.bfloat16)

def reference(tokens, gain, w_query, w_key, w_value, group_ids, key_pages, value_pages, page_table):
    values_wide = tokens.astype(jnp.float32)
    squares = lax.optimization_barrier(jnp.sum(values_wide * values_wide, axis=1, keepdims=True))
    normed = (values_wide * lax.rsqrt(squares / D + EPS) * gain.astype(jnp.float32)[None, :]).astype(jnp.bfloat16)
    query_all = jnp.dot(normed, w_query.reshape(D, KV * GQ * HD), preferred_element_type=jnp.float32).astype(jnp.bfloat16)
    key_all = jnp.dot(normed, w_key.reshape(D, KV * HD), preferred_element_type=jnp.float32).astype(jnp.bfloat16)
    value_all = jnp.dot(normed, w_value.reshape(D, KV * HD), preferred_element_type=jnp.float32).astype(jnp.bfloat16)
    group_of = group_ids[:, 0].astype(jnp.int32)
    member = (group_of[:, None] == jnp.arange(GROUPS, dtype=jnp.int32)[None, :]).astype(jnp.int32)
    token_rank = lax.optimization_barrier(jnp.sum((jnp.cumsum(member, axis=0) - member) * member, axis=1)).astype(jnp.int32)
    counts = lax.optimization_barrier(jnp.sum(member, axis=0)).astype(jnp.int32)
    starts = (jnp.cumsum(counts) - counts).astype(jnp.int32)
    order = jnp.argsort(group_of, stable=True).astype(jnp.int32)
    slot_total = N_TOK * CAP

    def one_group(group_index):
        place = jnp.arange(slot_total, dtype=jnp.int32)
        live = place < counts[group_index]
        chosen_rows = order[jnp.clip(starts[group_index] + place, 0, TOKENS - 1)]
        slot_rank = token_rank[chosen_rows]
        positions = (PREFIX + slot_rank).astype(jnp.int32)
        rotated_queries = rotate(query_all[chosen_rows].reshape(slot_total, KV * GQ, HD), positions).reshape(slot_total, KV, GQ, HD)
        rotated_keys = rotate(key_all[chosen_rows].reshape(slot_total, KV, HD), positions)
        slot_values = value_all[chosen_rows].reshape(slot_total, KV, HD)
        pages_used = page_table[group_index].astype(jnp.int32)
        prefix_keys = key_pages[pages_used].reshape(PREFIX, KV, HD)
        prefix_values = value_pages[pages_used].reshape(PREFIX, KV, HD)

        def one_head(head_index):
            return attend(rotated_queries[:, head_index], slot_rank, prefix_keys[:, head_index], prefix_values[:, head_index], rotated_keys[:, head_index], slot_values[:, head_index], slot_rank, live)
        result = lax.map(one_head, jnp.arange(KV, dtype=jnp.int32))
        result = jnp.transpose(result, (1, 0, 2, 3)).reshape(slot_total, KV * GQ * HD)
        return (result, jnp.where(live, chosen_rows, TOKENS).astype(jnp.int32))
    outputs, targets = lax.map(one_group, jnp.arange(GROUPS, dtype=jnp.int32))
    whole = jnp.zeros((TOKENS + 1, KV * GQ * HD), jnp.bfloat16)
    whole = whole.at[targets.reshape(-1)].set(outputs.reshape(GROUPS * slot_total, KV * GQ * HD))
    return whole[:TOKENS]
```

```python
import math

import jax
import jax.numpy as jnp
from jax import lax
from jax.sharding import PartitionSpec as P

EPS = 1e-05
THETA = 10000.0


def rotate(values, positions):
    halfway = values.shape[-1] // 2
    frequency = jnp.exp(
        -math.log(THETA) * 2.0 * jnp.arange(halfway, dtype=jnp.float32) / values.shape[-1]
    )
    angles = positions.astype(jnp.float32)[:, None] * frequency[None, :]
    cosine = jnp.cos(angles)[:, None, :]
    sine_part = jnp.sin(angles)[:, None, :]
    leading = values[..., :halfway].astype(jnp.float32)
    trailing = values[..., halfway:].astype(jnp.float32)
    return jnp.concatenate(
        [leading * cosine - trailing * sine_part, trailing * cosine + leading * sine_part], axis=-1
    ).astype(jnp.bfloat16)


def attend(
    queries, query_rank, prefix_keys, prefix_values, new_keys, new_values, key_rank, key_live
):
    scaling = 1.0 / math.sqrt(queries.shape[-1])
    before = (
        jnp.einsum("bhd,pd->bhp", queries, prefix_keys, preferred_element_type=jnp.float32)
        * scaling
    )
    inside = (
        jnp.einsum("bhd,sd->bhs", queries, new_keys, preferred_element_type=jnp.float32) * scaling
    )
    allowed = key_live[None, :] & (key_rank[None, :] <= query_rank[:, None])
    inside = jnp.where(allowed[:, None, :], inside, -jnp.inf)
    highest = jnp.maximum(jnp.max(before, axis=-1), jnp.max(inside, axis=-1))
    expo_before = jnp.exp(before - highest[..., None])
    expo_inside = jnp.exp(inside - highest[..., None])
    totals = jnp.sum(expo_before, axis=-1) + jnp.sum(expo_inside, axis=-1)
    mixed = jnp.einsum(
        "bhp,pd->bhd",
        expo_before.astype(jnp.bfloat16),
        prefix_values,
        preferred_element_type=jnp.float32,
    )
    mixed = mixed + jnp.einsum(
        "bhs,sd->bhd",
        expo_inside.astype(jnp.bfloat16),
        new_values,
        preferred_element_type=jnp.float32,
    )
    return (mixed / totals[..., None]).astype(jnp.bfloat16)


def row_norm(tokens, gain, full_width):
    values_wide = tokens.astype(jnp.float32)
    squares = lax.psum(jnp.sum(values_wide * values_wide, axis=1), "head")
    factor = lax.rsqrt(squares / full_width + EPS)
    return (values_wide * factor[:, None] * gain.astype(jnp.float32)[None, :]).astype(jnp.bfloat16)


def body(tokens, gain, w_query, w_key, w_value, group_ids, key_pages, value_pages, page_table):
    row_count = tokens.shape[0]
    n_tok = lax.axis_size("tok")
    n_head = lax.axis_size("head")
    head_size = key_pages.shape[-1]
    query_width = w_query.shape[2]
    group_heads = query_width // head_size
    full_width = tokens.shape[1] * n_head
    capacity = 2 * row_count // n_tok
    normed = row_norm(tokens, gain, full_width)
    weights_local = jnp.concatenate([w_query, w_key, w_value], axis=2)
    gathered = lax.all_gather(weights_local, "tok", axis=0, tiled=True)
    group_count = row_count * lax.axis_size("head") // row_count
    joined = jnp.einsum("rd,dnc->nrc", normed, gathered, preferred_element_type=jnp.float32)
    projected = lax.psum_scatter(
        joined.reshape(group_count * row_count, joined.shape[2]),
        "head",
        scatter_dimension=0,
        tiled=True,
    )
    projected_low = projected.astype(jnp.bfloat16)
    width_all = projected_low.shape[1]
    group_of = group_ids[:, 0]
    member = (group_of[:, None] == jnp.arange(n_tok, dtype=jnp.int32)[None, :]).astype(jnp.int32)
    local_rank = jnp.sum((jnp.cumsum(member, axis=0) - member) * member, axis=1)
    slot_index = group_of * capacity + local_rank
    outgoing = (
        jnp.zeros((n_tok * capacity, width_all), jnp.bfloat16).at[slot_index].set(projected_low)
    )
    arrived = lax.all_to_all(
        outgoing.reshape(n_tok, capacity, width_all),
        "tok",
        split_axis=0,
        concat_axis=0,
        tiled=True,
    )
    all_groups = lax.all_gather(group_of, "tok", axis=0, tiled=True).reshape(n_tok, row_count)
    block_counts = jnp.sum(
        (all_groups == lax.axis_index("tok")).astype(jnp.int32), axis=1
    )
    slot_total = n_tok * capacity
    arrived = arrived.reshape(slot_total, width_all)
    live_count = (
        jnp.arange(capacity, dtype=jnp.int32)[None, :] < block_counts[:, None]
    ).astype(jnp.int32).reshape(slot_total)
    key_live = live_count > 0
    slot_rank = jnp.cumsum(live_count) - live_count
    prefix_length = page_table.shape[1] * key_pages.shape[1]
    positions = prefix_length + slot_rank
    rotated_queries = rotate(
        arrived[:, :query_width].reshape(slot_total, group_heads, head_size), positions
    )
    rotated_keys = rotate(
        arrived[:, query_width : query_width + head_size].reshape(slot_total, 1, head_size),
        positions,
    )[:, 0, :]
    slot_values = arrived[:, query_width + head_size :]
    local_pages = page_table[0] - lax.axis_index("tok") * key_pages.shape[0]
    prefix_keys = jnp.take(key_pages[:, :, 0, :], local_pages, axis=0).reshape(
        prefix_length, head_size
    )
    prefix_values = jnp.take(value_pages[:, :, 0, :], local_pages, axis=0).reshape(
        prefix_length, head_size
    )
    block_size = min(128, slot_total)

    def one_block(blocked):
        return attend(
            blocked[0],
            blocked[1],
            prefix_keys,
            prefix_values,
            rotated_keys,
            slot_values,
            slot_rank,
            key_live,
        )

    attended = lax.map(
        one_block,
        (
            rotated_queries.reshape(slot_total // block_size, block_size, group_heads, head_size),
            slot_rank.reshape(slot_total // block_size, block_size),
        ),
    )
    returned = lax.all_to_all(
        attended.reshape(n_tok, capacity, query_width),
        "tok",
        split_axis=0,
        concat_axis=0,
        tiled=True,
    )
    return returned.reshape(n_tok * capacity, query_width)[slot_index]


def solution(mesh):
    placed = (
        P("tok", "head"),
        P("head"),
        P(("head", "tok"), None, None),
        P(("head", "tok"), None, None),
        P(("head", "tok"), None, None),
        P("tok", None),
        P("tok", None, "head", None),
        P("tok", None, "head", None),
        P("tok", None),
    )
    return jax.shard_map(
        body, mesh=mesh, in_specs=placed, out_specs=P("tok", "head"), check_vma=False
    )
```

```python
import math

import jax
import jax.numpy as jnp
from jax import lax
from jax.sharding import PartitionSpec as P

EPS = 1e-05
THETA = 10000.0


def rotate(values, positions):
    halfway = values.shape[-1] // 2
    frequency = jnp.exp(
        -math.log(THETA) * 2.0 * jnp.arange(halfway, dtype=jnp.float32) / values.shape[-1]
    )
    angles = positions.astype(jnp.float32)[:, None] * frequency[None, :]
    cosine = jnp.cos(angles)[:, None, :]
    sine_part = jnp.sin(angles)[:, None, :]
    leading = values[..., :halfway].astype(jnp.float32)
    trailing = values[..., halfway:].astype(jnp.float32)
    return jnp.concatenate(
        [leading * cosine - trailing * sine_part, trailing * cosine + leading * sine_part], axis=-1
    ).astype(jnp.bfloat16)


def attend(
    queries, query_rank, prefix_keys, prefix_values, new_keys, new_values, key_rank, key_live
):
    scaling = 1.0 / math.sqrt(queries.shape[-1])
    before = (
        jnp.einsum("bhd,pd->bhp", queries, prefix_keys, preferred_element_type=jnp.float32)
        * scaling
    )
    inside = (
        jnp.einsum("bhd,sd->bhs", queries, new_keys, preferred_element_type=jnp.float32) * scaling
    )
    allowed = key_live[None, :] & (key_rank[None, :] <= query_rank[:, None])
    inside = jnp.where(allowed[:, None, :], inside, -jnp.inf)
    highest = jnp.maximum(jnp.max(before, axis=-1), jnp.max(inside, axis=-1))
    expo_before = jnp.exp(before - highest[..., None])
    expo_inside = jnp.exp(inside - highest[..., None])
    totals = jnp.sum(expo_before, axis=-1) + jnp.sum(expo_inside, axis=-1)
    mixed = jnp.einsum(
        "bhp,pd->bhd",
        expo_before.astype(jnp.bfloat16),
        prefix_values,
        preferred_element_type=jnp.float32,
    )
    mixed = mixed + jnp.einsum(
        "bhs,sd->bhd",
        expo_inside.astype(jnp.bfloat16),
        new_values,
        preferred_element_type=jnp.float32,
    )
    return (mixed / totals[..., None]).astype(jnp.bfloat16)


def row_norm(tokens, gain, full_width):
    values_wide = tokens.astype(jnp.float32)
    squares = lax.psum(jnp.sum(values_wide * values_wide, axis=1), "head")
    factor = lax.rsqrt(squares / full_width + EPS)
    return (values_wide * factor[:, None] * gain.astype(jnp.float32)[None, :]).astype(jnp.bfloat16)


def body(tokens, gain, w_query, w_key, w_value, group_ids, key_pages, value_pages, page_table):
    row_count = tokens.shape[0]
    n_tok = lax.axis_size("tok")
    n_head = lax.axis_size("head")
    head_size = key_pages.shape[-1]
    query_width = w_query.shape[2]
    group_heads = query_width // head_size
    full_width = tokens.shape[1] * n_head
    capacity = 2 * row_count // n_tok
    normed = row_norm(tokens, gain, full_width)
    weights_local = jnp.concatenate([w_query, w_key, w_value], axis=2)
    gathered = lax.all_gather(weights_local, "tok", axis=0, tiled=True)
    group_count = row_count * lax.axis_size("head") // row_count
    joined = jnp.einsum("rd,dnc->nrc", normed, gathered, preferred_element_type=jnp.float32)
    projected = lax.psum_scatter(
        joined.reshape(group_count * row_count, joined.shape[2]),
        "head",
        scatter_dimension=0,
        tiled=True,
    )
    projected_low = projected.astype(jnp.bfloat16)
    width_all = projected_low.shape[1]
    group_of = group_ids[:, 0]
    member = (group_of[:, None] == jnp.arange(n_tok, dtype=jnp.int32)[None, :]).astype(jnp.int32)
    local_rank = jnp.sum((jnp.cumsum(member, axis=0) - member) * member, axis=1)
    slot_index = group_of * capacity + local_rank
    counts_local = jnp.sum(member, axis=0).astype(jnp.bfloat16)
    outgoing = (
        jnp.zeros((n_tok * capacity, width_all), jnp.bfloat16).at[slot_index].set(projected_low)
    )
    count_rows = jnp.broadcast_to(counts_local[:, None, None], (n_tok, 16, width_all))
    outgoing = jnp.concatenate(
        [outgoing.reshape(n_tok, capacity, width_all), count_rows], axis=1
    )
    arrived_all = lax.all_to_all(outgoing, "tok", split_axis=0, concat_axis=0, tiled=True)
    block_counts = arrived_all[:, capacity, 0].astype(jnp.int32)
    arrived = arrived_all[:, :capacity, :]
    slot_total = n_tok * capacity
    arrived = arrived.reshape(slot_total, width_all)
    live_count = (
        jnp.arange(capacity, dtype=jnp.int32)[None, :] < block_counts[:, None]
    ).astype(jnp.int32).reshape(slot_total)
    key_live = live_count > 0
    slot_rank = jnp.cumsum(live_count) - live_count
    prefix_length = page_table.shape[1] * key_pages.shape[1]
    positions = prefix_length + slot_rank
    rotated_queries = rotate(
        arrived[:, :query_width].reshape(slot_total, group_heads, head_size), positions
    )
    rotated_keys = rotate(
        arrived[:, query_width : query_width + head_size].reshape(slot_total, 1, head_size),
        positions,
    )[:, 0, :]
    slot_values = arrived[:, query_width + head_size :]
    local_pages = page_table[0] - lax.axis_index("tok") * key_pages.shape[0]
    prefix_keys = jnp.take(key_pages[:, :, 0, :], local_pages, axis=0).reshape(
        prefix_length, head_size
    )
    prefix_values = jnp.take(value_pages[:, :, 0, :], local_pages, axis=0).reshape(
        prefix_length, head_size
    )
    block_size = min(128, slot_total)

    def one_block(blocked):
        return attend(
            blocked[0],
            blocked[1],
            prefix_keys,
            prefix_values,
            rotated_keys,
            slot_values,
            slot_rank,
            key_live,
        )

    attended = lax.map(
        one_block,
        (
            rotated_queries.reshape(slot_total // block_size, block_size, group_heads, head_size),
            slot_rank.reshape(slot_total // block_size, block_size),
        ),
    )
    returned = lax.all_to_all(
        attended.reshape(n_tok, capacity, query_width),
        "tok",
        split_axis=0,
        concat_axis=0,
        tiled=True,
    )
    return returned.reshape(n_tok * capacity, query_width)[slot_index]


def solution(mesh):
    placed = (
        P("tok", "head"),
        P("head"),
        P(("head", "tok"), None, None),
        P(("head", "tok"), None, None),
        P(("head", "tok"), None, None),
        P("tok", None),
        P("tok", None, "head", None),
        P("tok", None, "head", None),
        P("tok", None),
    )
    return jax.shard_map(
        body, mesh=mesh, in_specs=placed, out_specs=P("tok", "head"), check_vma=False
    )
```

```python
import math

import jax
import jax.numpy as jnp
from jax import lax
from jax.experimental import pallas as pl
from jax.experimental.pallas import tpu as pltpu
from jax.sharding import PartitionSpec as P

EPS = 1e-05
THETA = 10000.0


def rotate(values, positions):
    halfway = values.shape[-1] // 2
    frequency = jnp.exp(
        -math.log(THETA) * 2.0 * jnp.arange(halfway, dtype=jnp.float32) / values.shape[-1]
    )
    angles = positions.astype(jnp.float32)[:, None] * frequency[None, :]
    cosine = jnp.cos(angles)[:, None, :]
    sine_part = jnp.sin(angles)[:, None, :]
    leading = values[..., :halfway].astype(jnp.float32)
    trailing = values[..., halfway:].astype(jnp.float32)
    return jnp.concatenate(
        [leading * cosine - trailing * sine_part, trailing * cosine + leading * sine_part], axis=-1
    ).astype(jnp.bfloat16)


def attend(
    queries, query_rank, prefix_keys, prefix_values, new_keys, new_values, key_rank, key_live
):
    scaling = 1.0 / math.sqrt(queries.shape[-1])
    before = (
        jnp.einsum("bhd,pd->bhp", queries, prefix_keys, preferred_element_type=jnp.float32)
        * scaling
    )
    inside = (
        jnp.einsum("bhd,sd->bhs", queries, new_keys, preferred_element_type=jnp.float32) * scaling
    )
    allowed = key_live[None, :] & (key_rank[None, :] <= query_rank[:, None])
    inside = jnp.where(allowed[:, None, :], inside, -jnp.inf)
    highest = jnp.maximum(jnp.max(before, axis=-1), jnp.max(inside, axis=-1))
    expo_before = jnp.exp(before - highest[..., None])
    expo_inside = jnp.exp(inside - highest[..., None])
    totals = jnp.sum(expo_before, axis=-1) + jnp.sum(expo_inside, axis=-1)
    mixed = jnp.einsum(
        "bhp,pd->bhd",
        expo_before.astype(jnp.bfloat16),
        prefix_values,
        preferred_element_type=jnp.float32,
    )
    mixed = mixed + jnp.einsum(
        "bhs,sd->bhd",
        expo_inside.astype(jnp.bfloat16),
        new_values,
        preferred_element_type=jnp.float32,
    )
    return (mixed / totals[..., None]).astype(jnp.bfloat16)


def attention_kernel(q_ref, qr_ref, kp_ref, vp_ref, kn_ref, vn_ref, kr_ref, o_ref):
    scaling = 1.0 / math.sqrt(q_ref.shape[-1])
    q = q_ref[...]
    before = lax.dot_general(
        q, kp_ref[...], (((1,), (1,)), ((), ())), preferred_element_type=jnp.float32
    ) * scaling
    inside = lax.dot_general(
        q, kn_ref[...], (((1,), (1,)), ((), ())), preferred_element_type=jnp.float32
    ) * scaling
    allowed = kr_ref[...] <= qr_ref[...]
    inside = jnp.where(allowed, inside, -jnp.inf)
    highest = jnp.maximum(
        jnp.max(before, axis=1, keepdims=True), jnp.max(inside, axis=1, keepdims=True)
    )
    expo_before = jnp.exp(before - highest)
    expo_inside = jnp.exp(inside - highest)
    totals = jnp.sum(expo_before, axis=1, keepdims=True) + jnp.sum(
        expo_inside, axis=1, keepdims=True
    )
    mixed = jnp.dot(
        expo_before.astype(jnp.bfloat16), vp_ref[...], preferred_element_type=jnp.float32
    ) + jnp.dot(
        expo_inside.astype(jnp.bfloat16), vn_ref[...], preferred_element_type=jnp.float32
    )
    o_ref[...] = (mixed / totals).astype(o_ref.dtype)


def attend_all(queries, query_rank, prefix_keys, prefix_values, new_keys, new_values,
               key_rank, key_live, block_rows=256):
    slots, heads, size = queries.shape
    rows = slots * heads
    q = queries.reshape(rows, size)
    q_rank = jnp.repeat(query_rank, heads).reshape(rows, 1)
    big = jnp.iinfo(jnp.int32).max
    k_rank = jnp.where(key_live, key_rank, big).reshape(1, -1)
    prefix_len = prefix_keys.shape[0]
    new_len = new_keys.shape[0]
    full = lambda i: (0, 0)
    out = pl.pallas_call(
        attention_kernel,
        grid=(rows // block_rows,),
        in_specs=[
            pl.BlockSpec((block_rows, size), lambda i: (i, 0)),
            pl.BlockSpec((block_rows, 1), lambda i: (i, 0)),
            pl.BlockSpec((prefix_len, size), full),
            pl.BlockSpec((prefix_len, size), full),
            pl.BlockSpec((new_len, size), full),
            pl.BlockSpec((new_len, size), full),
            pl.BlockSpec((1, new_len), full),
        ],
        out_specs=pl.BlockSpec((block_rows, size), lambda i: (i, 0)),
        out_shape=jax.ShapeDtypeStruct((rows, size), jnp.bfloat16),
        compiler_params=pltpu.CompilerParams(vmem_limit_bytes=48 * 1024 * 1024),
    )(q, q_rank, prefix_keys, prefix_values, new_keys, new_values, k_rank)
    return out.reshape(slots, heads, size)


def row_norm(tokens, gain, full_width):
    values_wide = tokens.astype(jnp.float32)
    squares = lax.psum(jnp.sum(values_wide * values_wide, axis=1), "head")
    factor = lax.rsqrt(squares / full_width + EPS)
    return (values_wide * factor[:, None] * gain.astype(jnp.float32)[None, :]).astype(jnp.bfloat16)


def body(tokens, gain, w_query, w_key, w_value, group_ids, key_pages, value_pages, page_table):
    row_count = tokens.shape[0]
    n_tok = lax.axis_size("tok")
    n_head = lax.axis_size("head")
    head_size = key_pages.shape[-1]
    query_width = w_query.shape[2]
    group_heads = query_width // head_size
    full_width = tokens.shape[1] * n_head
    capacity = 2 * row_count // n_tok
    normed = row_norm(tokens, gain, full_width)
    weights_local = jnp.concatenate([w_query, w_key, w_value], axis=2)
    gathered = lax.all_gather(weights_local, "tok", axis=0, tiled=True)
    group_count = row_count * lax.axis_size("head") // row_count
    joined = jnp.einsum("rd,dnc->nrc", normed, gathered, preferred_element_type=jnp.float32)
    projected = lax.psum_scatter(
        joined.reshape(group_count * row_count, joined.shape[2]),
        "head",
        scatter_dimension=0,
        tiled=True,
    )
    projected_low = projected.astype(jnp.bfloat16)
    width_all = projected_low.shape[1]
    group_of = group_ids[:, 0]
    member = (group_of[:, None] == jnp.arange(n_tok, dtype=jnp.int32)[None, :]).astype(jnp.int32)
    local_rank = jnp.sum((jnp.cumsum(member, axis=0) - member) * member, axis=1)
    slot_index = group_of * capacity + local_rank
    counts_local = jnp.sum(member, axis=0).astype(jnp.bfloat16)
    outgoing = (
        jnp.zeros((n_tok * capacity, width_all), jnp.bfloat16).at[slot_index].set(projected_low)
    )
    count_rows = jnp.broadcast_to(counts_local[:, None, None], (n_tok, 16, width_all))
    outgoing = jnp.concatenate(
        [outgoing.reshape(n_tok, capacity, width_all), count_rows], axis=1
    )
    arrived_all = lax.all_to_all(outgoing, "tok", split_axis=0, concat_axis=0, tiled=True)
    block_counts = arrived_all[:, capacity, 0].astype(jnp.int32)
    arrived = arrived_all[:, :capacity, :]
    slot_total = n_tok * capacity
    arrived = arrived.reshape(slot_total, width_all)
    live_count = (
        jnp.arange(capacity, dtype=jnp.int32)[None, :] < block_counts[:, None]
    ).astype(jnp.int32).reshape(slot_total)
    key_live = live_count > 0
    slot_rank = jnp.cumsum(live_count) - live_count
    prefix_length = page_table.shape[1] * key_pages.shape[1]
    positions = prefix_length + slot_rank
    rotated_queries = rotate(
        arrived[:, :query_width].reshape(slot_total, group_heads, head_size), positions
    )
    rotated_keys = rotate(
        arrived[:, query_width : query_width + head_size].reshape(slot_total, 1, head_size),
        positions,
    )[:, 0, :]
    slot_values = arrived[:, query_width + head_size :]
    local_pages = page_table[0] - lax.axis_index("tok") * key_pages.shape[0]
    prefix_keys = jnp.take(key_pages[:, :, 0, :], local_pages, axis=0).reshape(
        prefix_length, head_size
    )
    prefix_values = jnp.take(value_pages[:, :, 0, :], local_pages, axis=0).reshape(
        prefix_length, head_size
    )
    attended = attend_all(
        rotated_queries,
        slot_rank,
        prefix_keys,
        prefix_values,
        rotated_keys,
        slot_values,
        slot_rank,
        key_live,
    )
    returned = lax.all_to_all(
        attended.reshape(n_tok, capacity, query_width),
        "tok",
        split_axis=0,
        concat_axis=0,
        tiled=True,
    )
    return returned.reshape(n_tok * capacity, query_width)[slot_index]


def solution(mesh):
    placed = (
        P("tok", "head"),
        P("head"),
        P(("head", "tok"), None, None),
        P(("head", "tok"), None, None),
        P(("head", "tok"), None, None),
        P("tok", None),
        P("tok", None, "head", None),
        P("tok", None, "head", None),
        P("tok", None),
    )
    return jax.shard_map(
        body, mesh=mesh, in_specs=placed, out_specs=P("tok", "head"), check_vma=False
    )
```

```python
import math

import jax
import jax.numpy as jnp
from jax import lax
from jax.experimental import pallas as pl
from jax.experimental.pallas import tpu as pltpu
from jax.sharding import PartitionSpec as P

EPS = 1e-05
THETA = 10000.0


def rotate(values, positions):
    halfway = values.shape[-1] // 2
    frequency = jnp.exp(
        -math.log(THETA) * 2.0 * jnp.arange(halfway, dtype=jnp.float32) / values.shape[-1]
    )
    angles = positions.astype(jnp.float32)[:, None] * frequency[None, :]
    cosine = jnp.cos(angles)[:, None, :]
    sine_part = jnp.sin(angles)[:, None, :]
    leading = values[..., :halfway].astype(jnp.float32)
    trailing = values[..., halfway:].astype(jnp.float32)
    return jnp.concatenate(
        [leading * cosine - trailing * sine_part, trailing * cosine + leading * sine_part], axis=-1
    ).astype(jnp.bfloat16)


def attend(
    queries, query_rank, prefix_keys, prefix_values, new_keys, new_values, key_rank, key_live
):
    scaling = 1.0 / math.sqrt(queries.shape[-1])
    before = (
        jnp.einsum("bhd,pd->bhp", queries, prefix_keys, preferred_element_type=jnp.float32)
        * scaling
    )
    inside = (
        jnp.einsum("bhd,sd->bhs", queries, new_keys, preferred_element_type=jnp.float32) * scaling
    )
    allowed = key_live[None, :] & (key_rank[None, :] <= query_rank[:, None])
    inside = jnp.where(allowed[:, None, :], inside, -jnp.inf)
    highest = jnp.maximum(jnp.max(before, axis=-1), jnp.max(inside, axis=-1))
    expo_before = jnp.exp(before - highest[..., None])
    expo_inside = jnp.exp(inside - highest[..., None])
    totals = jnp.sum(expo_before, axis=-1) + jnp.sum(expo_inside, axis=-1)
    mixed = jnp.einsum(
        "bhp,pd->bhd",
        expo_before.astype(jnp.bfloat16),
        prefix_values,
        preferred_element_type=jnp.float32,
    )
    mixed = mixed + jnp.einsum(
        "bhs,sd->bhd",
        expo_inside.astype(jnp.bfloat16),
        new_values,
        preferred_element_type=jnp.float32,
    )
    return (mixed / totals[..., None]).astype(jnp.bfloat16)


def attention_kernel(q_ref, qr_ref, kp_ref, vp_ref, kn_ref, vn_ref, kr_ref, o_ref):
    scaling = 1.0 / math.sqrt(q_ref.shape[-1])
    q = q_ref[...]
    before = lax.dot_general(
        q, kp_ref[...], (((1,), (1,)), ((), ())), preferred_element_type=jnp.float32
    ) * scaling
    inside = lax.dot_general(
        q, kn_ref[...], (((1,), (1,)), ((), ())), preferred_element_type=jnp.float32
    ) * scaling
    allowed = kr_ref[...] <= qr_ref[...]
    inside = jnp.where(allowed, inside, -jnp.inf)
    highest = jnp.maximum(
        jnp.max(before, axis=1, keepdims=True), jnp.max(inside, axis=1, keepdims=True)
    )
    expo_before = jnp.exp(before - highest)
    expo_inside = jnp.exp(inside - highest)
    totals = jnp.sum(expo_before, axis=1, keepdims=True) + jnp.sum(
        expo_inside, axis=1, keepdims=True
    )
    mixed = jnp.dot(
        expo_before.astype(jnp.bfloat16), vp_ref[...], preferred_element_type=jnp.float32
    ) + jnp.dot(
        expo_inside.astype(jnp.bfloat16), vn_ref[...], preferred_element_type=jnp.float32
    )
    o_ref[...] = (mixed / totals).astype(o_ref.dtype)


def attend_all(queries, query_rank, prefix_keys, prefix_values, new_keys, new_values,
               key_rank, key_live, block_rows=256):
    slots, heads, size = queries.shape
    rows = slots * heads
    q = queries.reshape(rows, size)
    q_rank = jnp.repeat(query_rank, heads).reshape(rows, 1)
    big = jnp.iinfo(jnp.int32).max
    k_rank = jnp.where(key_live, key_rank, big).reshape(1, -1)
    prefix_len = prefix_keys.shape[0]
    new_len = new_keys.shape[0]
    full = lambda i: (0, 0)
    out = pl.pallas_call(
        attention_kernel,
        grid=(rows // block_rows,),
        in_specs=[
            pl.BlockSpec((block_rows, size), lambda i: (i, 0)),
            pl.BlockSpec((block_rows, 1), lambda i: (i, 0)),
            pl.BlockSpec((prefix_len, size), full),
            pl.BlockSpec((prefix_len, size), full),
            pl.BlockSpec((new_len, size), full),
            pl.BlockSpec((new_len, size), full),
            pl.BlockSpec((1, new_len), full),
        ],
        out_specs=pl.BlockSpec((block_rows, size), lambda i: (i, 0)),
        out_shape=jax.ShapeDtypeStruct((rows, size), jnp.bfloat16),
        compiler_params=pltpu.CompilerParams(vmem_limit_bytes=48 * 1024 * 1024),
    )(q, q_rank, prefix_keys, prefix_values, new_keys, new_values, k_rank)
    return out.reshape(slots, heads, size)


def row_norm(tokens, gain, full_width):
    values_wide = tokens.astype(jnp.float32)
    squares = lax.psum(jnp.sum(values_wide * values_wide, axis=1), "head")
    factor = lax.rsqrt(squares / full_width + EPS)
    return (values_wide * factor[:, None] * gain.astype(jnp.float32)[None, :]).astype(jnp.bfloat16)


def pair_order(own, other, parity):
    stacked = jnp.stack([own, other])
    return jnp.take(stacked, jnp.stack([parity, 1 - parity]), axis=0)


def body(tokens, gain, w_query, w_key, w_value, group_ids, key_pages, value_pages, page_table):
    row_count = tokens.shape[0]
    n_pair = lax.axis_size("tp")
    n_tok = n_pair * 2
    n_head = lax.axis_size("head")
    head_size = key_pages.shape[-1]
    query_width = w_query.shape[2]
    group_heads = query_width // head_size
    half_heads = group_heads // 2
    full_width = tokens.shape[1] * n_head
    capacity = 2 * row_count // n_tok
    pair_capacity = 2 * capacity
    parity = lax.axis_index("tq")
    tok_index = lax.axis_index("tp") * 2 + parity
    swap = [(0, 1), (1, 0)]
    normed = row_norm(tokens, gain, full_width)
    weights_local = jnp.concatenate([w_query, w_key, w_value], axis=2)
    split_q = half_heads * head_size
    first_half = jnp.concatenate(
        [weights_local[:, :, :split_q], weights_local[:, :, query_width : query_width + head_size]],
        axis=2,
    )
    second_half = jnp.concatenate(
        [weights_local[:, :, split_q:query_width], weights_local[:, :, query_width + head_size :]],
        axis=2,
    )
    keep = jnp.where(parity == 0, first_half, second_half)
    send = jnp.where(parity == 0, second_half, first_half)
    received = lax.ppermute(send, "tq", swap)
    pair_weights = pair_order(keep, received, parity)
    pair_weights = pair_weights.reshape((-1,) + pair_weights.shape[2:])
    gathered = lax.all_gather(pair_weights, "tp", axis=0, tiled=True)
    partner_normed = lax.ppermute(normed, "tq", swap)
    pair_normed = pair_order(normed, partner_normed, parity).reshape(2 * row_count, -1)
    group_own = group_ids[:, 0]
    group_partner = lax.ppermute(group_own, "tq", swap)
    group_pair = pair_order(group_own, group_partner, parity).reshape(2 * row_count)
    joined = jnp.einsum("rd,dnc->nrc", pair_normed, gathered, preferred_element_type=jnp.float32)
    projected = lax.psum_scatter(
        joined.reshape(n_head * 2 * row_count, joined.shape[2]),
        "head",
        scatter_dimension=0,
        tiled=True,
    )
    projected_low = projected.astype(jnp.bfloat16)
    width_half = projected_low.shape[1]
    member = (group_pair[:, None] == jnp.arange(n_tok, dtype=jnp.int32)[None, :]).astype(jnp.int32)
    pair_rank = jnp.sum((jnp.cumsum(member, axis=0) - member) * member, axis=1)
    slot_index = group_pair * pair_capacity + pair_rank
    counts_first = jnp.sum(member[:row_count], axis=0).astype(jnp.bfloat16)
    counts_second = jnp.sum(member[row_count:], axis=0).astype(jnp.bfloat16)
    outgoing = (
        jnp.zeros((n_tok * pair_capacity, width_half), jnp.bfloat16)
        .at[slot_index]
        .set(projected_low)
    )
    count_rows = jnp.zeros((n_tok, 16, width_half), jnp.bfloat16)
    count_rows = count_rows.at[:, 0, :].set(counts_first[:, None])
    count_rows = count_rows.at[:, 1, :].set(counts_second[:, None])
    outgoing = jnp.concatenate(
        [outgoing.reshape(n_tok, pair_capacity, width_half), count_rows], axis=1
    )
    arrived_all = lax.all_to_all(outgoing, ("tp", "tq"), 0, 0, tiled=True)
    arrived_all = arrived_all.reshape(n_pair, 2, pair_capacity + 16, width_half)
    count_first = arrived_all[:, 0, pair_capacity, 0].astype(jnp.int32)
    count_second = arrived_all[:, 0, pair_capacity + 1, 0].astype(jnp.int32)
    part_one = arrived_all[:, 0, :pair_capacity, :]
    part_two = arrived_all[:, 1, :pair_capacity, :]
    slot_total = n_pair * pair_capacity
    slot_queries = jnp.concatenate(
        [part_one[..., :split_q], part_two[..., :split_q]], axis=-1
    ).reshape(slot_total, group_heads, head_size)
    slot_keys = part_one[..., split_q:].reshape(slot_total, 1, head_size)
    slot_values = part_two[..., split_q:].reshape(slot_total, head_size)
    live_count = (
        jnp.arange(pair_capacity, dtype=jnp.int32)[None, :]
        < (count_first + count_second)[:, None]
    ).astype(jnp.int32).reshape(slot_total)
    key_live = live_count > 0
    slot_rank = jnp.cumsum(live_count) - live_count
    prefix_length = page_table.shape[1] * key_pages.shape[1]
    positions = prefix_length + slot_rank
    rotated_queries = rotate(slot_queries, positions)
    rotated_keys = rotate(slot_keys, positions)[:, 0, :]
    local_pages = page_table[0] - tok_index * key_pages.shape[0]
    prefix_keys = jnp.take(key_pages[:, :, 0, :], local_pages, axis=0).reshape(
        prefix_length, head_size
    )
    prefix_values = jnp.take(value_pages[:, :, 0, :], local_pages, axis=0).reshape(
        prefix_length, head_size
    )
    attended = attend_all(
        rotated_queries,
        slot_rank,
        prefix_keys,
        prefix_values,
        rotated_keys,
        slot_values,
        slot_rank,
        key_live,
    ).reshape(n_pair, pair_capacity, query_width)
    later = jnp.clip(
        count_first[:, None] + jnp.arange(capacity, dtype=jnp.int32)[None, :],
        0,
        pair_capacity - 1,
    )
    back = jnp.stack(
        [attended[:, :capacity, :], jnp.take_along_axis(attended, later[:, :, None], axis=1)],
        axis=1,
    )
    returned = lax.all_to_all(
        back.reshape(n_tok, capacity, query_width), ("tp", "tq"), 0, 0, tiled=True
    )
    member_own = member[:row_count] * (1 - parity) + member[row_count:] * parity
    group_of = group_own
    local_rank = jnp.sum((jnp.cumsum(member_own, axis=0) - member_own) * member_own, axis=1)
    return returned.reshape(n_tok * capacity, query_width)[group_of * capacity + local_rank]


def solution(mesh):
    n_tok, n_head = mesh.devices.shape
    paired = jax.sharding.Mesh(
        mesh.devices.reshape(n_tok // 2, 2, n_head), ("tp", "tq", "head")
    )
    tok = ("tp", "tq")
    placed = (
        P(tok, "head"),
        P("head"),
        P(("head",) + tok, None, None),
        P(("head",) + tok, None, None),
        P(("head",) + tok, None, None),
        P(tok, None),
        P(tok, None, "head", None),
        P(tok, None, "head", None),
        P(tok, None),
    )
    return jax.shard_map(
        body, mesh=paired, in_specs=placed, out_specs=P(tok, "head"), check_vma=False
    )
```

```python
import math

import jax
import jax.numpy as jnp
from jax import lax
from jax.experimental import pallas as pl
from jax.experimental.pallas import tpu as pltpu
from jax.sharding import PartitionSpec as P

EPS = 1e-05
THETA = 10000.0


def rotate(values, positions):
    halfway = values.shape[-1] // 2
    frequency = jnp.exp(
        -math.log(THETA) * 2.0 * jnp.arange(halfway, dtype=jnp.float32) / values.shape[-1]
    )
    angles = positions.astype(jnp.float32)[:, None] * frequency[None, :]
    cosine = jnp.cos(angles)[:, None, :]
    sine_part = jnp.sin(angles)[:, None, :]
    leading = values[..., :halfway].astype(jnp.float32)
    trailing = values[..., halfway:].astype(jnp.float32)
    return jnp.concatenate(
        [leading * cosine - trailing * sine_part, trailing * cosine + leading * sine_part], axis=-1
    ).astype(jnp.bfloat16)


def attend(
    queries, query_rank, prefix_keys, prefix_values, new_keys, new_values, key_rank, key_live
):
    scaling = 1.0 / math.sqrt(queries.shape[-1])
    before = (
        jnp.einsum("bhd,pd->bhp", queries, prefix_keys, preferred_element_type=jnp.float32)
        * scaling
    )
    inside = (
        jnp.einsum("bhd,sd->bhs", queries, new_keys, preferred_element_type=jnp.float32) * scaling
    )
    allowed = key_live[None, :] & (key_rank[None, :] <= query_rank[:, None])
    inside = jnp.where(allowed[:, None, :], inside, -jnp.inf)
    highest = jnp.maximum(jnp.max(before, axis=-1), jnp.max(inside, axis=-1))
    expo_before = jnp.exp(before - highest[..., None])
    expo_inside = jnp.exp(inside - highest[..., None])
    totals = jnp.sum(expo_before, axis=-1) + jnp.sum(expo_inside, axis=-1)
    mixed = jnp.einsum(
        "bhp,pd->bhd",
        expo_before.astype(jnp.bfloat16),
        prefix_values,
        preferred_element_type=jnp.float32,
    )
    mixed = mixed + jnp.einsum(
        "bhs,sd->bhd",
        expo_inside.astype(jnp.bfloat16),
        new_values,
        preferred_element_type=jnp.float32,
    )
    return (mixed / totals[..., None]).astype(jnp.bfloat16)


def attention_kernel(q_ref, cos_ref, sin_ref, qr_ref, kp_ref, vp_ref, kn_ref, vn_ref, kr_ref, o_ref):
    size = kp_ref.shape[-1]
    heads = q_ref.shape[-1] // size
    scaling = 1.0 / math.sqrt(size)
    cosine = cos_ref[...]
    sine = sin_ref[...]
    parts = []
    for head in range(heads):
        wide = q_ref[:, head * size : (head + 1) * size].astype(jnp.float32)
        turned = pltpu.roll(wide, size // 2, 1)
        parts.append((wide * cosine + turned * sine).astype(jnp.bfloat16))
    q = jnp.concatenate(parts, axis=0)
    q_rank = jnp.concatenate([qr_ref[...]] * heads, axis=0)
    before = lax.dot_general(
        q, kp_ref[...], (((1,), (1,)), ((), ())), preferred_element_type=jnp.float32
    ) * scaling
    inside = lax.dot_general(
        q, kn_ref[...], (((1,), (1,)), ((), ())), preferred_element_type=jnp.float32
    ) * scaling
    inside = jnp.where(kr_ref[...] <= q_rank, inside, -jnp.inf)
    highest = jnp.maximum(
        jnp.max(before, axis=1, keepdims=True), jnp.max(inside, axis=1, keepdims=True)
    )
    expo_before = jnp.exp(before - highest)
    expo_inside = jnp.exp(inside - highest)
    totals = jnp.sum(expo_before, axis=1, keepdims=True) + jnp.sum(
        expo_inside, axis=1, keepdims=True
    )
    mixed = jnp.dot(
        expo_before.astype(jnp.bfloat16), vp_ref[...], preferred_element_type=jnp.float32
    ) + jnp.dot(
        expo_inside.astype(jnp.bfloat16), vn_ref[...], preferred_element_type=jnp.float32
    )
    result = (mixed / totals).astype(o_ref.dtype)
    rows = q_ref.shape[0]
    for head in range(heads):
        o_ref[:, head * size : (head + 1) * size] = result[head * rows : (head + 1) * rows]


def attend_rotating(queries, positions, query_rank, prefix_keys, prefix_values, new_keys,
                    new_values, key_rank, key_live, block_slots=64):
    slots, width = queries.shape
    size = prefix_keys.shape[-1]
    halfway = size // 2
    frequency = jnp.exp(
        -math.log(10000.0) * 2.0 * jnp.arange(halfway, dtype=jnp.float32) / size
    )
    angles = positions.astype(jnp.float32)[:, None] * frequency[None, :]
    cosine = jnp.cos(angles)
    sine = jnp.sin(angles)
    cos_table = jnp.concatenate([cosine, cosine], axis=1)
    sin_table = jnp.concatenate([-sine, sine], axis=1)
    big = jnp.iinfo(jnp.int32).max
    k_rank = jnp.where(key_live, key_rank, big).reshape(1, -1)
    prefix_len = prefix_keys.shape[0]
    new_len = new_keys.shape[0]
    full = lambda i: (0, 0)
    by_slot = lambda i: (i, 0)
    return pl.pallas_call(
        attention_kernel,
        grid=(slots // block_slots,),
        in_specs=[
            pl.BlockSpec((block_slots, width), by_slot),
            pl.BlockSpec((block_slots, size), by_slot),
            pl.BlockSpec((block_slots, size), by_slot),
            pl.BlockSpec((block_slots, 1), by_slot),
            pl.BlockSpec((prefix_len, size), full),
            pl.BlockSpec((prefix_len, size), full),
            pl.BlockSpec((new_len, size), full),
            pl.BlockSpec((new_len, size), full),
            pl.BlockSpec((1, new_len), full),
        ],
        out_specs=pl.BlockSpec((block_slots, width), by_slot),
        out_shape=jax.ShapeDtypeStruct((slots, width), jnp.bfloat16),
        compiler_params=pltpu.CompilerParams(vmem_limit_bytes=48 * 1024 * 1024),
    )(queries, cos_table, sin_table, query_rank.reshape(slots, 1), prefix_keys, prefix_values,
      new_keys, new_values, k_rank)


def row_norm(tokens, gain, full_width):
    values_wide = tokens.astype(jnp.float32)
    squares = lax.psum(jnp.sum(values_wide * values_wide, axis=1), "head")
    factor = lax.rsqrt(squares / full_width + EPS)
    return (values_wide * factor[:, None] * gain.astype(jnp.float32)[None, :]).astype(jnp.bfloat16)


def body(tokens, gain, w_query, w_key, w_value, group_ids, key_pages, value_pages, page_table):
    row_count = tokens.shape[0]
    n_tok = lax.axis_size("tok")
    n_head = lax.axis_size("head")
    head_size = key_pages.shape[-1]
    query_width = w_query.shape[2]
    group_heads = query_width // head_size
    full_width = tokens.shape[1] * n_head
    capacity = 2 * row_count // n_tok
    normed = row_norm(tokens, gain, full_width)
    weights_local = jnp.concatenate([w_query, w_key, w_value], axis=2)
    gathered = lax.all_gather(weights_local, "tok", axis=0, tiled=True)
    group_count = row_count * lax.axis_size("head") // row_count
    joined = jnp.einsum("rd,dnc->nrc", normed, gathered, preferred_element_type=jnp.float32)
    projected = lax.psum_scatter(
        joined.reshape(group_count * row_count, joined.shape[2]),
        "head",
        scatter_dimension=0,
        tiled=True,
    )
    projected_low = projected.astype(jnp.bfloat16)
    width_all = projected_low.shape[1]
    group_of = group_ids[:, 0]
    member = (group_of[:, None] == jnp.arange(n_tok, dtype=jnp.int32)[None, :]).astype(jnp.int32)
    local_rank = jnp.sum((jnp.cumsum(member, axis=0) - member) * member, axis=1)
    slot_index = group_of * capacity + local_rank
    counts_local = jnp.sum(member, axis=0).astype(jnp.bfloat16)
    outgoing = (
        jnp.zeros((n_tok * capacity, width_all), jnp.bfloat16).at[slot_index].set(projected_low)
    )
    count_rows = jnp.broadcast_to(counts_local[:, None, None], (n_tok, 16, width_all))
    outgoing = jnp.concatenate(
        [outgoing.reshape(n_tok, capacity, width_all), count_rows], axis=1
    )
    arrived_all = lax.all_to_all(outgoing, "tok", split_axis=0, concat_axis=0, tiled=True)
    block_counts = arrived_all[:, capacity, 0].astype(jnp.int32)
    arrived = arrived_all[:, :capacity, :]
    slot_total = n_tok * capacity
    arrived = arrived.reshape(slot_total, width_all)
    live_count = (
        jnp.arange(capacity, dtype=jnp.int32)[None, :] < block_counts[:, None]
    ).astype(jnp.int32).reshape(slot_total)
    key_live = live_count > 0
    slot_rank = jnp.cumsum(live_count) - live_count
    prefix_length = page_table.shape[1] * key_pages.shape[1]
    positions = prefix_length + slot_rank
    rotated_keys = rotate(
        arrived[:, query_width : query_width + head_size].reshape(slot_total, 1, head_size),
        positions,
    )[:, 0, :]
    slot_values = arrived[:, query_width + head_size :]
    local_pages = page_table[0] - lax.axis_index("tok") * key_pages.shape[0]
    prefix_keys = jnp.take(key_pages[:, :, 0, :], local_pages, axis=0).reshape(
        prefix_length, head_size
    )
    prefix_values = jnp.take(value_pages[:, :, 0, :], local_pages, axis=0).reshape(
        prefix_length, head_size
    )
    attended = attend_rotating(
        arrived[:, :query_width],
        positions,
        slot_rank,
        prefix_keys,
        prefix_values,
        rotated_keys,
        slot_values,
        slot_rank,
        key_live,
    )
    returned = lax.all_to_all(
        attended.reshape(n_tok, capacity, query_width),
        "tok",
        split_axis=0,
        concat_axis=0,
        tiled=True,
    )
    return returned.reshape(n_tok * capacity, query_width)[slot_index]


def solution(mesh):
    placed = (
        P("tok", "head"),
        P("head"),
        P(("head", "tok"), None, None),
        P(("head", "tok"), None, None),
        P(("head", "tok"), None, None),
        P("tok", None),
        P("tok", None, "head", None),
        P("tok", None, "head", None),
        P("tok", None),
    )
    return jax.shard_map(
        body, mesh=mesh, in_specs=placed, out_specs=P("tok", "head"), check_vma=False
    )
```

```python
import math

import jax
import jax.numpy as jnp
from jax import lax
from jax.experimental import pallas as pl
from jax.experimental.pallas import tpu as pltpu
from jax.sharding import PartitionSpec as P

EPS = 1e-05
THETA = 10000.0


def rotate(values, positions):
    halfway = values.shape[-1] // 2
    frequency = jnp.exp(
        -math.log(THETA) * 2.0 * jnp.arange(halfway, dtype=jnp.float32) / values.shape[-1]
    )
    angles = positions.astype(jnp.float32)[:, None] * frequency[None, :]
    cosine = jnp.cos(angles)[:, None, :]
    sine_part = jnp.sin(angles)[:, None, :]
    leading = values[..., :halfway].astype(jnp.float32)
    trailing = values[..., halfway:].astype(jnp.float32)
    return jnp.concatenate(
        [leading * cosine - trailing * sine_part, trailing * cosine + leading * sine_part], axis=-1
    ).astype(jnp.bfloat16)


def attend(
    queries, query_rank, prefix_keys, prefix_values, new_keys, new_values, key_rank, key_live
):
    scaling = 1.0 / math.sqrt(queries.shape[-1])
    before = (
        jnp.einsum("bhd,pd->bhp", queries, prefix_keys, preferred_element_type=jnp.float32)
        * scaling
    )
    inside = (
        jnp.einsum("bhd,sd->bhs", queries, new_keys, preferred_element_type=jnp.float32) * scaling
    )
    allowed = key_live[None, :] & (key_rank[None, :] <= query_rank[:, None])
    inside = jnp.where(allowed[:, None, :], inside, -jnp.inf)
    highest = jnp.maximum(jnp.max(before, axis=-1), jnp.max(inside, axis=-1))
    expo_before = jnp.exp(before - highest[..., None])
    expo_inside = jnp.exp(inside - highest[..., None])
    totals = jnp.sum(expo_before, axis=-1) + jnp.sum(expo_inside, axis=-1)
    mixed = jnp.einsum(
        "bhp,pd->bhd",
        expo_before.astype(jnp.bfloat16),
        prefix_values,
        preferred_element_type=jnp.float32,
    )
    mixed = mixed + jnp.einsum(
        "bhs,sd->bhd",
        expo_inside.astype(jnp.bfloat16),
        new_values,
        preferred_element_type=jnp.float32,
    )
    return (mixed / totals[..., None]).astype(jnp.bfloat16)


def attention_kernel(q_ref, cos_ref, sin_ref, qr_ref, kp_ref, vp_ref, kn_ref, vn_ref, kr_ref, o_ref):
    size = kp_ref.shape[-1]
    heads = q_ref.shape[-1] // size
    scaling = 1.0 / math.sqrt(size)
    cosine = cos_ref[...]
    sine = sin_ref[...]
    parts = []
    for head in range(heads):
        wide = q_ref[:, head * size : (head + 1) * size].astype(jnp.float32)
        turned = pltpu.roll(wide, size // 2, 1)
        parts.append((wide * cosine + turned * sine).astype(jnp.bfloat16))
    q = jnp.concatenate(parts, axis=0)
    q_rank = jnp.concatenate([qr_ref[...]] * heads, axis=0)
    before = lax.dot_general(
        q, kp_ref[...], (((1,), (1,)), ((), ())), preferred_element_type=jnp.float32
    ) * scaling
    inside = lax.dot_general(
        q, kn_ref[...], (((1,), (1,)), ((), ())), preferred_element_type=jnp.float32
    ) * scaling
    inside = jnp.where(kr_ref[...] <= q_rank, inside, -jnp.inf)
    highest = jnp.maximum(
        jnp.max(before, axis=1, keepdims=True), jnp.max(inside, axis=1, keepdims=True)
    )
    expo_before = jnp.exp(before - highest)
    expo_inside = jnp.exp(inside - highest)
    totals = jnp.sum(expo_before, axis=1, keepdims=True) + jnp.sum(
        expo_inside, axis=1, keepdims=True
    )
    mixed = jnp.dot(
        expo_before.astype(jnp.bfloat16), vp_ref[...], preferred_element_type=jnp.float32
    ) + jnp.dot(
        expo_inside.astype(jnp.bfloat16), vn_ref[...], preferred_element_type=jnp.float32
    )
    result = (mixed / totals).astype(o_ref.dtype)
    rows = q_ref.shape[0]
    for head in range(heads):
        o_ref[:, head * size : (head + 1) * size] = result[head * rows : (head + 1) * rows]


def attend_rotating(arrived, width, positions, query_rank, prefix_keys, prefix_values, new_keys,
                    key_rank, key_live, block_slots=64):
    slots = arrived.shape[0]
    size = prefix_keys.shape[-1]
    halfway = size // 2
    frequency = jnp.exp(
        -math.log(10000.0) * 2.0 * jnp.arange(halfway, dtype=jnp.float32) / size
    )
    angles = positions.astype(jnp.float32)[:, None] * frequency[None, :]
    cosine = jnp.cos(angles)
    sine = jnp.sin(angles)
    cos_table = jnp.concatenate([cosine, cosine], axis=1)
    sin_table = jnp.concatenate([-sine, sine], axis=1)
    big = jnp.iinfo(jnp.int32).max
    k_rank = jnp.where(key_live, key_rank, big).reshape(1, -1)
    prefix_len = prefix_keys.shape[0]
    new_len = new_keys.shape[0]
    full = lambda i: (0, 0)
    by_slot = lambda i: (i, 0)
    return pl.pallas_call(
        attention_kernel,
        grid=(slots // block_slots,),
        in_specs=[
            pl.BlockSpec((block_slots, width), by_slot),
            pl.BlockSpec((block_slots, size), by_slot),
            pl.BlockSpec((block_slots, size), by_slot),
            pl.BlockSpec((block_slots, 1), by_slot),
            pl.BlockSpec((prefix_len, size), full),
            pl.BlockSpec((prefix_len, size), full),
            pl.BlockSpec((new_len, size), full),
            pl.BlockSpec((new_len, size), lambda i: (0, width // size + 1)),
            pl.BlockSpec((1, new_len), full),
        ],
        out_specs=pl.BlockSpec((block_slots, width), by_slot),
        out_shape=jax.ShapeDtypeStruct((slots, width), jnp.bfloat16),
        compiler_params=pltpu.CompilerParams(vmem_limit_bytes=48 * 1024 * 1024),
    )(arrived, cos_table, sin_table, query_rank.reshape(slots, 1), prefix_keys, prefix_values,
      new_keys, arrived, k_rank)


def row_norm(tokens, gain, full_width):
    values_wide = tokens.astype(jnp.float32)
    squares = lax.psum(jnp.sum(values_wide * values_wide, axis=1), "head")
    factor = lax.rsqrt(squares / full_width + EPS)
    return (values_wide * factor[:, None] * gain.astype(jnp.float32)[None, :]).astype(jnp.bfloat16)


def body(tokens, gain, w_query, w_key, w_value, group_ids, key_pages, value_pages, page_table):
    row_count = tokens.shape[0]
    n_tok = lax.axis_size("tok")
    n_head = lax.axis_size("head")
    head_size = key_pages.shape[-1]
    query_width = w_query.shape[2]
    group_heads = query_width // head_size
    full_width = tokens.shape[1] * n_head
    capacity = 2 * row_count // n_tok
    normed = row_norm(tokens, gain, full_width)
    weights_local = jnp.concatenate([w_query, w_key, w_value], axis=2)
    gathered = lax.all_gather(weights_local, "tok", axis=0, tiled=True)
    group_count = row_count * lax.axis_size("head") // row_count
    joined = jnp.einsum("rd,dnc->nrc", normed, gathered, preferred_element_type=jnp.float32)
    projected = lax.psum_scatter(
        joined.reshape(group_count * row_count, joined.shape[2]),
        "head",
        scatter_dimension=0,
        tiled=True,
    )
    projected_low = projected.astype(jnp.bfloat16)
    width_all = projected_low.shape[1]
    group_of = group_ids[:, 0]
    member = (group_of[:, None] == jnp.arange(n_tok, dtype=jnp.int32)[None, :]).astype(jnp.int32)
    local_rank = jnp.sum((jnp.cumsum(member, axis=0) - member) * member, axis=1)
    slot_index = group_of * capacity + local_rank
    counts_local = jnp.sum(member, axis=0).reshape(n_tok, 1)
    block_counts = lax.all_to_all(counts_local, "tok", 0, 0, tiled=True).reshape(n_tok)
    outgoing = (
        jnp.zeros((n_tok * capacity, width_all), jnp.bfloat16).at[slot_index].set(projected_low)
    )
    arrived = lax.all_to_all(
        outgoing.reshape(n_tok, capacity, width_all), "tok", 0, 0, tiled=True
    )
    slot_total = n_tok * capacity
    arrived = arrived.reshape(slot_total, width_all)
    live_count = (
        jnp.arange(capacity, dtype=jnp.int32)[None, :] < block_counts[:, None]
    ).astype(jnp.int32).reshape(slot_total)
    key_live = live_count > 0
    slot_rank = jnp.cumsum(live_count) - live_count
    prefix_length = page_table.shape[1] * key_pages.shape[1]
    positions = prefix_length + slot_rank
    rotated_keys = rotate(
        arrived[:, query_width : query_width + head_size].reshape(slot_total, 1, head_size),
        positions,
    )[:, 0, :]
    local_pages = page_table[0] - lax.axis_index("tok") * key_pages.shape[0]
    prefix_keys = jnp.take(key_pages[:, :, 0, :], local_pages, axis=0).reshape(
        prefix_length, head_size
    )
    prefix_values = jnp.take(value_pages[:, :, 0, :], local_pages, axis=0).reshape(
        prefix_length, head_size
    )
    attended = attend_rotating(
        arrived,
        query_width,
        positions,
        slot_rank,
        prefix_keys,
        prefix_values,
        rotated_keys,
        slot_rank,
        key_live,
    )
    returned = lax.all_to_all(
        attended.reshape(n_tok, capacity, query_width),
        "tok",
        split_axis=0,
        concat_axis=0,
        tiled=True,
    )
    return returned.reshape(n_tok * capacity, query_width)[slot_index]


def solution(mesh):
    placed = (
        P("tok", "head"),
        P("head"),
        P(("head", "tok"), None, None),
        P(("head", "tok"), None, None),
        P(("head", "tok"), None, None),
        P("tok", None),
        P("tok", None, "head", None),
        P("tok", None, "head", None),
        P("tok", None),
    )
    return jax.shard_map(
        body, mesh=mesh, in_specs=placed, out_specs=P("tok", "head"), check_vma=False
    )
```

```python
import math

import jax
import jax.numpy as jnp
from jax import lax
from jax.experimental import pallas as pl
from jax.experimental.pallas import tpu as pltpu
from jax.sharding import PartitionSpec as P

EPS = 1e-05
THETA = 10000.0


def rotate(values, positions):
    halfway = values.shape[-1] // 2
    frequency = jnp.exp(
        -math.log(THETA) * 2.0 * jnp.arange(halfway, dtype=jnp.float32) / values.shape[-1]
    )
    angles = positions.astype(jnp.float32)[:, None] * frequency[None, :]
    cosine = jnp.cos(angles)[:, None, :]
    sine_part = jnp.sin(angles)[:, None, :]
    leading = values[..., :halfway].astype(jnp.float32)
    trailing = values[..., halfway:].astype(jnp.float32)
    return jnp.concatenate(
        [leading * cosine - trailing * sine_part, trailing * cosine + leading * sine_part], axis=-1
    ).astype(jnp.bfloat16)


def attend(
    queries, query_rank, prefix_keys, prefix_values, new_keys, new_values, key_rank, key_live
):
    scaling = 1.0 / math.sqrt(queries.shape[-1])
    before = (
        jnp.einsum("bhd,pd->bhp", queries, prefix_keys, preferred_element_type=jnp.float32)
        * scaling
    )
    inside = (
        jnp.einsum("bhd,sd->bhs", queries, new_keys, preferred_element_type=jnp.float32) * scaling
    )
    allowed = key_live[None, :] & (key_rank[None, :] <= query_rank[:, None])
    inside = jnp.where(allowed[:, None, :], inside, -jnp.inf)
    highest = jnp.maximum(jnp.max(before, axis=-1), jnp.max(inside, axis=-1))
    expo_before = jnp.exp(before - highest[..., None])
    expo_inside = jnp.exp(inside - highest[..., None])
    totals = jnp.sum(expo_before, axis=-1) + jnp.sum(expo_inside, axis=-1)
    mixed = jnp.einsum(
        "bhp,pd->bhd",
        expo_before.astype(jnp.bfloat16),
        prefix_values,
        preferred_element_type=jnp.float32,
    )
    mixed = mixed + jnp.einsum(
        "bhs,sd->bhd",
        expo_inside.astype(jnp.bfloat16),
        new_values,
        preferred_element_type=jnp.float32,
    )
    return (mixed / totals[..., None]).astype(jnp.bfloat16)


def attention_kernel(q_ref, cos_ref, sin_ref, qr_ref, kp_ref, vp_ref, kn_ref, vn_ref, kr_ref, o_ref):
    size = kp_ref.shape[-1]
    heads = q_ref.shape[-1] // size
    scaling = 1.0 / math.sqrt(size)
    cosine = cos_ref[...]
    sine = sin_ref[...]
    parts = []
    for head in range(heads):
        wide = q_ref[:, head * size : (head + 1) * size].astype(jnp.float32)
        turned = pltpu.roll(wide, size // 2, 1)
        parts.append((wide * cosine + turned * sine).astype(jnp.bfloat16))
    q = jnp.concatenate(parts, axis=0)
    q_rank = jnp.concatenate([qr_ref[...]] * heads, axis=0)
    before = lax.dot_general(
        q, kp_ref[...], (((1,), (1,)), ((), ())), preferred_element_type=jnp.float32
    ) * scaling
    inside = lax.dot_general(
        q, kn_ref[...], (((1,), (1,)), ((), ())), preferred_element_type=jnp.float32
    ) * scaling
    inside = jnp.where(kr_ref[...] <= q_rank, inside, -jnp.inf)
    highest = jnp.maximum(
        jnp.max(before, axis=1, keepdims=True), jnp.max(inside, axis=1, keepdims=True)
    )
    expo_before = jnp.exp(before - highest)
    expo_inside = jnp.exp(inside - highest)
    totals = jnp.sum(expo_before, axis=1, keepdims=True) + jnp.sum(
        expo_inside, axis=1, keepdims=True
    )
    mixed = jnp.dot(
        expo_before.astype(jnp.bfloat16), vp_ref[...], preferred_element_type=jnp.float32
    ) + jnp.dot(
        expo_inside.astype(jnp.bfloat16), vn_ref[...], preferred_element_type=jnp.float32
    )
    result = (mixed / totals).astype(o_ref.dtype)
    rows = q_ref.shape[0]
    for head in range(heads):
        o_ref[:, head * size : (head + 1) * size] = result[head * rows : (head + 1) * rows]


def attend_rotating(arrived, width, positions, query_rank, prefix_keys, prefix_values, new_keys,
                    key_rank, key_live, block_slots=64):
    slots = arrived.shape[0]
    size = prefix_keys.shape[-1]
    halfway = size // 2
    frequency = jnp.exp(
        -math.log(10000.0) * 2.0 * jnp.arange(halfway, dtype=jnp.float32) / size
    )
    angles = positions.astype(jnp.float32)[:, None] * frequency[None, :]
    cosine = jnp.cos(angles)
    sine = jnp.sin(angles)
    cos_table = jnp.concatenate([cosine, cosine], axis=1)
    sin_table = jnp.concatenate([-sine, sine], axis=1)
    big = jnp.iinfo(jnp.int32).max
    k_rank = jnp.where(key_live, key_rank, big).reshape(1, -1)
    prefix_len = prefix_keys.shape[0]
    new_len = new_keys.shape[0]
    full = lambda i: (0, 0)
    by_slot = lambda i: (i, 0)
    return pl.pallas_call(
        attention_kernel,
        grid=(slots // block_slots,),
        in_specs=[
            pl.BlockSpec((block_slots, width), by_slot),
            pl.BlockSpec((block_slots, size), by_slot),
            pl.BlockSpec((block_slots, size), by_slot),
            pl.BlockSpec((block_slots, 1), by_slot),
            pl.BlockSpec((prefix_len, size), full),
            pl.BlockSpec((prefix_len, size), full),
            pl.BlockSpec((new_len, size), full),
            pl.BlockSpec((new_len, size), lambda i: (0, width // size + 1)),
            pl.BlockSpec((1, new_len), full),
        ],
        out_specs=pl.BlockSpec((block_slots, width), by_slot),
        out_shape=jax.ShapeDtypeStruct((slots, width), jnp.bfloat16),
        compiler_params=pltpu.CompilerParams(vmem_limit_bytes=48 * 1024 * 1024),
    )(arrived, cos_table, sin_table, query_rank.reshape(slots, 1), prefix_keys, prefix_values,
      new_keys, arrived, k_rank)


def row_norm(tokens, gain, full_width):
    values_wide = tokens.astype(jnp.float32)
    squares = lax.psum(jnp.sum(values_wide * values_wide, axis=1), "head")
    factor = lax.rsqrt(squares / full_width + EPS)
    return (values_wide * factor[:, None] * gain.astype(jnp.float32)[None, :]).astype(jnp.bfloat16)


def body(tokens, gain, w_query, w_key, w_value, group_ids, key_pages, value_pages, page_table):
    row_count = tokens.shape[0]
    n_tok = lax.axis_size("tok")
    n_head = lax.axis_size("head")
    head_size = key_pages.shape[-1]
    query_width = w_query.shape[2]
    group_heads = query_width // head_size
    full_width = tokens.shape[1] * n_head
    capacity = 2 * row_count // n_tok
    weights_local = jnp.concatenate([w_query, w_key, w_value], axis=2)
    weights_head = lax.all_to_all(weights_local, "head", 1, 0, tiled=True)
    weights_head = weights_head.reshape(n_head, -1, weights_head.shape[-1])
    gathered = lax.all_gather(weights_head, "tok", axis=1, tiled=True)
    gathered = gathered.reshape(-1, gathered.shape[-1])
    gain_rows = jnp.broadcast_to(gain[None, :], (16, gain.shape[0]))
    stacked = lax.all_gather(
        jnp.concatenate([tokens, gain_rows], axis=0), "head", axis=1, tiled=True
    )
    tokens_full = stacked[:row_count]
    gain_full = stacked[row_count]
    values_wide = tokens_full.astype(jnp.float32)
    squares = jnp.sum(values_wide * values_wide, axis=1)
    factor = lax.rsqrt(squares / full_width + EPS)
    normed = (values_wide * factor[:, None] * gain_full.astype(jnp.float32)[None, :]).astype(
        jnp.bfloat16
    )
    projected = jnp.dot(normed, gathered, preferred_element_type=jnp.float32)
    projected_low = projected.astype(jnp.bfloat16)
    width_all = projected_low.shape[1]
    group_of = group_ids[:, 0]
    member = (group_of[:, None] == jnp.arange(n_tok, dtype=jnp.int32)[None, :]).astype(jnp.int32)
    local_rank = jnp.sum((jnp.cumsum(member, axis=0) - member) * member, axis=1)
    slot_index = group_of * capacity + local_rank
    counts_local = jnp.sum(member, axis=0).reshape(n_tok, 1)
    block_counts = lax.all_to_all(counts_local, "tok", 0, 0, tiled=True).reshape(n_tok)
    outgoing = (
        jnp.zeros((n_tok * capacity, width_all), jnp.bfloat16).at[slot_index].set(projected_low)
    )
    arrived = lax.all_to_all(
        outgoing.reshape(n_tok, capacity, width_all), "tok", 0, 0, tiled=True
    )
    slot_total = n_tok * capacity
    arrived = arrived.reshape(slot_total, width_all)
    live_count = (
        jnp.arange(capacity, dtype=jnp.int32)[None, :] < block_counts[:, None]
    ).astype(jnp.int32).reshape(slot_total)
    key_live = live_count > 0
    slot_rank = jnp.cumsum(live_count) - live_count
    prefix_length = page_table.shape[1] * key_pages.shape[1]
    positions = prefix_length + slot_rank
    rotated_keys = rotate(
        arrived[:, query_width : query_width + head_size].reshape(slot_total, 1, head_size),
        positions,
    )[:, 0, :]
    local_pages = page_table[0] - lax.axis_index("tok") * key_pages.shape[0]
    prefix_keys = jnp.take(key_pages[:, :, 0, :], local_pages, axis=0).reshape(
        prefix_length, head_size
    )
    prefix_values = jnp.take(value_pages[:, :, 0, :], local_pages, axis=0).reshape(
        prefix_length, head_size
    )
    attended = attend_rotating(
        arrived,
        query_width,
        positions,
        slot_rank,
        prefix_keys,
        prefix_values,
        rotated_keys,
        slot_rank,
        key_live,
    )
    returned = lax.all_to_all(
        attended.reshape(n_tok, capacity, query_width),
        "tok",
        split_axis=0,
        concat_axis=0,
        tiled=True,
    )
    return returned.reshape(n_tok * capacity, query_width)[slot_index]


def solution(mesh):
    placed = (
        P("tok", "head"),
        P("head"),
        P(("head", "tok"), None, None),
        P(("head", "tok"), None, None),
        P(("head", "tok"), None, None),
        P("tok", None),
        P("tok", None, "head", None),
        P("tok", None, "head", None),
        P("tok", None),
    )
    return jax.shard_map(
        body, mesh=mesh, in_specs=placed, out_specs=P("tok", "head"), check_vma=False
    )
```

```python
import math

import jax
import jax.numpy as jnp
from jax import lax
from jax.experimental import pallas as pl
from jax.experimental.pallas import tpu as pltpu
from jax.sharding import PartitionSpec as P

EPS = 1e-05
THETA = 10000.0


def rotate(values, positions):
    halfway = values.shape[-1] // 2
    frequency = jnp.exp(
        -math.log(THETA) * 2.0 * jnp.arange(halfway, dtype=jnp.float32) / values.shape[-1]
    )
    angles = positions.astype(jnp.float32)[:, None] * frequency[None, :]
    cosine = jnp.cos(angles)[:, None, :]
    sine_part = jnp.sin(angles)[:, None, :]
    leading = values[..., :halfway].astype(jnp.float32)
    trailing = values[..., halfway:].astype(jnp.float32)
    return jnp.concatenate(
        [leading * cosine - trailing * sine_part, trailing * cosine + leading * sine_part], axis=-1
    ).astype(jnp.bfloat16)


def attend(
    queries, query_rank, prefix_keys, prefix_values, new_keys, new_values, key_rank, key_live
):
    scaling = 1.0 / math.sqrt(queries.shape[-1])
    before = (
        jnp.einsum("bhd,pd->bhp", queries, prefix_keys, preferred_element_type=jnp.float32)
        * scaling
    )
    inside = (
        jnp.einsum("bhd,sd->bhs", queries, new_keys, preferred_element_type=jnp.float32) * scaling
    )
    allowed = key_live[None, :] & (key_rank[None, :] <= query_rank[:, None])
    inside = jnp.where(allowed[:, None, :], inside, -jnp.inf)
    highest = jnp.maximum(jnp.max(before, axis=-1), jnp.max(inside, axis=-1))
    expo_before = jnp.exp(before - highest[..., None])
    expo_inside = jnp.exp(inside - highest[..., None])
    totals = jnp.sum(expo_before, axis=-1) + jnp.sum(expo_inside, axis=-1)
    mixed = jnp.einsum(
        "bhp,pd->bhd",
        expo_before.astype(jnp.bfloat16),
        prefix_values,
        preferred_element_type=jnp.float32,
    )
    mixed = mixed + jnp.einsum(
        "bhs,sd->bhd",
        expo_inside.astype(jnp.bfloat16),
        new_values,
        preferred_element_type=jnp.float32,
    )
    return (mixed / totals[..., None]).astype(jnp.bfloat16)


def attention_kernel(q_ref, cos_ref, sin_ref, qr_ref, kp_ref, vp_ref, kn_ref, vn_ref, kr_ref, o_ref):
    size = kp_ref.shape[-1]
    heads = q_ref.shape[-1] // size
    scaling = 1.0 / math.sqrt(size)
    cosine = cos_ref[...]
    sine = sin_ref[...]
    parts = []
    for head in range(heads):
        wide = q_ref[:, head * size : (head + 1) * size].astype(jnp.float32)
        turned = pltpu.roll(wide, size // 2, 1)
        parts.append((wide * cosine + turned * sine).astype(jnp.bfloat16))
    q = jnp.concatenate(parts, axis=0)
    q_rank = jnp.concatenate([qr_ref[...]] * heads, axis=0)
    before = lax.dot_general(
        q, kp_ref[...], (((1,), (1,)), ((), ())), preferred_element_type=jnp.float32
    ) * scaling
    inside = lax.dot_general(
        q, kn_ref[...], (((1,), (1,)), ((), ())), preferred_element_type=jnp.float32
    ) * scaling
    inside = jnp.where(kr_ref[...] <= q_rank, inside, -jnp.inf)
    highest = jnp.maximum(
        jnp.max(before, axis=1, keepdims=True), jnp.max(inside, axis=1, keepdims=True)
    )
    expo_before = jnp.exp(before - highest)
    expo_inside = jnp.exp(inside - highest)
    totals = jnp.sum(expo_before, axis=1, keepdims=True) + jnp.sum(
        expo_inside, axis=1, keepdims=True
    )
    mixed = jnp.dot(
        expo_before.astype(jnp.bfloat16), vp_ref[...], preferred_element_type=jnp.float32
    ) + jnp.dot(
        expo_inside.astype(jnp.bfloat16), vn_ref[...], preferred_element_type=jnp.float32
    )
    result = (mixed / totals).astype(o_ref.dtype)
    rows = q_ref.shape[0]
    for head in range(heads):
        o_ref[:, head * size : (head + 1) * size] = result[head * rows : (head + 1) * rows]


def attend_rotating(arrived, width, positions, query_rank, prefix_keys, prefix_values, new_keys,
                    key_rank, key_live, block_slots=64):
    slots = arrived.shape[0]
    size = prefix_keys.shape[-1]
    halfway = size // 2
    frequency = jnp.exp(
        -math.log(10000.0) * 2.0 * jnp.arange(halfway, dtype=jnp.float32) / size
    )
    angles = positions.astype(jnp.float32)[:, None] * frequency[None, :]
    cosine = jnp.cos(angles)
    sine = jnp.sin(angles)
    cos_table = jnp.concatenate([cosine, cosine], axis=1)
    sin_table = jnp.concatenate([-sine, sine], axis=1)
    big = jnp.iinfo(jnp.int32).max
    k_rank = jnp.where(key_live, key_rank, big).reshape(1, -1)
    prefix_len = prefix_keys.shape[0]
    new_len = new_keys.shape[0]
    full = lambda i: (0, 0)
    by_slot = lambda i: (i, 0)
    return pl.pallas_call(
        attention_kernel,
        grid=(slots // block_slots,),
        in_specs=[
            pl.BlockSpec((block_slots, width), by_slot),
            pl.BlockSpec((block_slots, size), by_slot),
            pl.BlockSpec((block_slots, size), by_slot),
            pl.BlockSpec((block_slots, 1), by_slot),
            pl.BlockSpec((prefix_len, size), full),
            pl.BlockSpec((prefix_len, size), full),
            pl.BlockSpec((new_len, size), full),
            pl.BlockSpec((new_len, size), lambda i: (0, width // size + 1)),
            pl.BlockSpec((1, new_len), full),
        ],
        out_specs=pl.BlockSpec((block_slots, width), by_slot),
        out_shape=jax.ShapeDtypeStruct((slots, width), jnp.bfloat16),
        compiler_params=pltpu.CompilerParams(vmem_limit_bytes=48 * 1024 * 1024),
    )(arrived, cos_table, sin_table, query_rank.reshape(slots, 1), prefix_keys, prefix_values,
      new_keys, arrived, k_rank)


def row_norm(tokens, gain, full_width):
    values_wide = tokens.astype(jnp.float32)
    squares = lax.psum(jnp.sum(values_wide * values_wide, axis=1), "head")
    factor = lax.rsqrt(squares / full_width + EPS)
    return (values_wide * factor[:, None] * gain.astype(jnp.float32)[None, :]).astype(jnp.bfloat16)


def body(tokens, gain, w_query, w_key, w_value, group_ids, key_pages, value_pages, page_table):
    row_count = tokens.shape[0]
    n_tok = lax.axis_size("tok")
    n_head = lax.axis_size("head")
    head_size = key_pages.shape[-1]
    query_width = w_query.shape[2]
    group_heads = query_width // head_size
    full_width = tokens.shape[1] * n_head
    capacity = 2 * row_count // n_tok
    weights_local = jnp.concatenate([w_query, w_key, w_value], axis=2)
    weights_head = lax.all_to_all(weights_local, "head", 1, 0, tiled=True)
    weights_head = weights_head.reshape(n_head, -1, weights_head.shape[-1])
    gathered = lax.all_gather(weights_head, "tok", axis=1, tiled=True)
    gathered = gathered.reshape(-1, gathered.shape[-1])
    gain_rows = jnp.broadcast_to(gain[None, :], (16, gain.shape[0]))
    stacked = lax.all_to_all(
        jnp.tile(jnp.concatenate([tokens, gain_rows], axis=0), (1, n_head)),
        "head",
        1,
        1,
        tiled=True,
    )
    tokens_full = stacked[:row_count]
    gain_full = stacked[row_count]
    values_wide = tokens_full.astype(jnp.float32)
    squares = jnp.sum(values_wide * values_wide, axis=1)
    factor = lax.rsqrt(squares / full_width + EPS)
    normed = (values_wide * factor[:, None] * gain_full.astype(jnp.float32)[None, :]).astype(
        jnp.bfloat16
    )
    projected = jnp.dot(normed, gathered, preferred_element_type=jnp.float32)
    projected_low = projected.astype(jnp.bfloat16)
    width_all = projected_low.shape[1]
    group_of = group_ids[:, 0]
    member = (group_of[:, None] == jnp.arange(n_tok, dtype=jnp.int32)[None, :]).astype(jnp.int32)
    local_rank = jnp.sum((jnp.cumsum(member, axis=0) - member) * member, axis=1)
    slot_index = group_of * capacity + local_rank
    counts_local = jnp.sum(member, axis=0).reshape(n_tok, 1)
    block_counts = lax.all_to_all(counts_local, "tok", 0, 0, tiled=True).reshape(n_tok)
    outgoing = (
        jnp.zeros((n_tok * capacity, width_all), jnp.bfloat16).at[slot_index].set(projected_low)
    )
    arrived = lax.all_to_all(
        outgoing.reshape(n_tok, capacity, width_all), "tok", 0, 0, tiled=True
    )
    slot_total = n_tok * capacity
    arrived = arrived.reshape(slot_total, width_all)
    live_count = (
        jnp.arange(capacity, dtype=jnp.int32)[None, :] < block_counts[:, None]
    ).astype(jnp.int32).reshape(slot_total)
    key_live = live_count > 0
    slot_rank = jnp.cumsum(live_count) - live_count
    prefix_length = page_table.shape[1] * key_pages.shape[1]
    positions = prefix_length + slot_rank
    rotated_keys = rotate(
        arrived[:, query_width : query_width + head_size].reshape(slot_total, 1, head_size),
        positions,
    )[:, 0, :]
    local_pages = page_table[0] - lax.axis_index("tok") * key_pages.shape[0]
    prefix_keys = jnp.take(key_pages[:, :, 0, :], local_pages, axis=0).reshape(
        prefix_length, head_size
    )
    prefix_values = jnp.take(value_pages[:, :, 0, :], local_pages, axis=0).reshape(
        prefix_length, head_size
    )
    attended = attend_rotating(
        arrived,
        query_width,
        positions,
        slot_rank,
        prefix_keys,
        prefix_values,
        rotated_keys,
        slot_rank,
        key_live,
    )
    returned = lax.all_to_all(
        attended.reshape(n_tok, capacity, query_width),
        "tok",
        split_axis=0,
        concat_axis=0,
        tiled=True,
    )
    return returned.reshape(n_tok * capacity, query_width)[slot_index]


def solution(mesh):
    placed = (
        P("tok", "head"),
        P("head"),
        P(("head", "tok"), None, None),
        P(("head", "tok"), None, None),
        P(("head", "tok"), None, None),
        P("tok", None),
        P("tok", None, "head", None),
        P("tok", None, "head", None),
        P("tok", None),
    )
    return jax.shard_map(
        body, mesh=mesh, in_specs=placed, out_specs=P("tok", "head"), check_vma=False
    )
```

```python
import math

import jax
import jax.numpy as jnp
from jax import lax
from jax.experimental import pallas as pl
from jax.experimental.pallas import tpu as pltpu
from jax.sharding import PartitionSpec as P

EPS = 1e-05
THETA = 10000.0


def rotate(values, positions):
    halfway = values.shape[-1] // 2
    frequency = jnp.exp(
        -math.log(THETA) * 2.0 * jnp.arange(halfway, dtype=jnp.float32) / values.shape[-1]
    )
    angles = positions.astype(jnp.float32)[:, None] * frequency[None, :]
    cosine = jnp.cos(angles)[:, None, :]
    sine_part = jnp.sin(angles)[:, None, :]
    leading = values[..., :halfway].astype(jnp.float32)
    trailing = values[..., halfway:].astype(jnp.float32)
    return jnp.concatenate(
        [leading * cosine - trailing * sine_part, trailing * cosine + leading * sine_part], axis=-1
    ).astype(jnp.bfloat16)


def attend(
    queries, query_rank, prefix_keys, prefix_values, new_keys, new_values, key_rank, key_live
):
    scaling = 1.0 / math.sqrt(queries.shape[-1])
    before = (
        jnp.einsum("bhd,pd->bhp", queries, prefix_keys, preferred_element_type=jnp.float32)
        * scaling
    )
    inside = (
        jnp.einsum("bhd,sd->bhs", queries, new_keys, preferred_element_type=jnp.float32) * scaling
    )
    allowed = key_live[None, :] & (key_rank[None, :] <= query_rank[:, None])
    inside = jnp.where(allowed[:, None, :], inside, -jnp.inf)
    highest = jnp.maximum(jnp.max(before, axis=-1), jnp.max(inside, axis=-1))
    expo_before = jnp.exp(before - highest[..., None])
    expo_inside = jnp.exp(inside - highest[..., None])
    totals = jnp.sum(expo_before, axis=-1) + jnp.sum(expo_inside, axis=-1)
    mixed = jnp.einsum(
        "bhp,pd->bhd",
        expo_before.astype(jnp.bfloat16),
        prefix_values,
        preferred_element_type=jnp.float32,
    )
    mixed = mixed + jnp.einsum(
        "bhs,sd->bhd",
        expo_inside.astype(jnp.bfloat16),
        new_values,
        preferred_element_type=jnp.float32,
    )
    return (mixed / totals[..., None]).astype(jnp.bfloat16)


def attention_kernel(q_ref, cos_ref, sin_ref, qr_ref, kp_ref, vp_ref, kn_ref, vn_ref, kr_ref, o_ref):
    size = kp_ref.shape[-1]
    heads = q_ref.shape[-1] // size
    scaling = 1.0 / math.sqrt(size)
    cosine = cos_ref[...]
    sine = sin_ref[...]
    parts = []
    for head in range(heads):
        wide = q_ref[:, head * size : (head + 1) * size].astype(jnp.float32)
        turned = pltpu.roll(wide, size // 2, 1)
        parts.append((wide * cosine + turned * sine).astype(jnp.bfloat16))
    q = jnp.concatenate(parts, axis=0)
    q_rank = jnp.concatenate([qr_ref[...]] * heads, axis=0)
    before = lax.dot_general(
        q, kp_ref[...], (((1,), (1,)), ((), ())), preferred_element_type=jnp.float32
    ) * scaling
    inside = lax.dot_general(
        q, kn_ref[...], (((1,), (1,)), ((), ())), preferred_element_type=jnp.float32
    ) * scaling
    inside = jnp.where(kr_ref[...] <= q_rank, inside, -jnp.inf)
    highest = jnp.maximum(
        jnp.max(before, axis=1, keepdims=True), jnp.max(inside, axis=1, keepdims=True)
    )
    expo_before = jnp.exp(before - highest)
    expo_inside = jnp.exp(inside - highest)
    totals = jnp.sum(expo_before, axis=1, keepdims=True) + jnp.sum(
        expo_inside, axis=1, keepdims=True
    )
    mixed = jnp.dot(
        expo_before.astype(jnp.bfloat16), vp_ref[...], preferred_element_type=jnp.float32
    ) + jnp.dot(
        expo_inside.astype(jnp.bfloat16), vn_ref[...], preferred_element_type=jnp.float32
    )
    result = (mixed / totals).astype(o_ref.dtype)
    rows = q_ref.shape[0]
    for head in range(heads):
        o_ref[:, head * size : (head + 1) * size] = result[head * rows : (head + 1) * rows]


def attend_rotating(arrived, width, positions, query_rank, prefix_keys, prefix_values, new_keys,
                    key_rank, key_live, block_slots=64):
    slots = arrived.shape[0]
    size = prefix_keys.shape[-1]
    halfway = size // 2
    frequency = jnp.exp(
        -math.log(10000.0) * 2.0 * jnp.arange(halfway, dtype=jnp.float32) / size
    )
    angles = positions.astype(jnp.float32)[:, None] * frequency[None, :]
    cosine = jnp.cos(angles)
    sine = jnp.sin(angles)
    cos_table = jnp.concatenate([cosine, cosine], axis=1)
    sin_table = jnp.concatenate([-sine, sine], axis=1)
    big = jnp.iinfo(jnp.int32).max
    k_rank = jnp.where(key_live, key_rank, big).reshape(1, -1)
    prefix_len = prefix_keys.shape[0]
    new_len = new_keys.shape[0]
    full = lambda i: (0, 0)
    by_slot = lambda i: (i, 0)
    return pl.pallas_call(
        attention_kernel,
        grid=(slots // block_slots,),
        in_specs=[
            pl.BlockSpec((block_slots, width), by_slot),
            pl.BlockSpec((block_slots, size), by_slot),
            pl.BlockSpec((block_slots, size), by_slot),
            pl.BlockSpec((block_slots, 1), by_slot),
            pl.BlockSpec((prefix_len, size), full),
            pl.BlockSpec((prefix_len, size), full),
            pl.BlockSpec((new_len, size), full),
            pl.BlockSpec((new_len, size), lambda i: (0, width // size + 1)),
            pl.BlockSpec((1, new_len), full),
        ],
        out_specs=pl.BlockSpec((block_slots, width), by_slot),
        out_shape=jax.ShapeDtypeStruct((slots, width), jnp.bfloat16),
        compiler_params=pltpu.CompilerParams(vmem_limit_bytes=48 * 1024 * 1024),
    )(arrived, cos_table, sin_table, query_rank.reshape(slots, 1), prefix_keys, prefix_values,
      new_keys, arrived, k_rank)


def row_norm(tokens, gain, full_width):
    values_wide = tokens.astype(jnp.float32)
    squares = lax.psum(jnp.sum(values_wide * values_wide, axis=1), "head")
    factor = lax.rsqrt(squares / full_width + EPS)
    return (values_wide * factor[:, None] * gain.astype(jnp.float32)[None, :]).astype(jnp.bfloat16)


def body(tokens, gain, w_query, w_key, w_value, group_ids, key_pages, value_pages, page_table):
    row_count = tokens.shape[0]
    n_tok = lax.axis_size("tok")
    n_head = lax.axis_size(("hz", "hc"))
    head_size = key_pages.shape[-1]
    query_width = w_query.shape[2]
    group_heads = query_width // head_size
    full_width = tokens.shape[1] * n_head
    capacity = 2 * row_count // n_tok
    weights_local = jnp.concatenate([w_query, w_key, w_value], axis=2)
    weights_head = lax.all_to_all(weights_local, ("hz", "hc"), 1, 0, tiled=True)
    weights_head = weights_head.reshape(n_head, -1, weights_head.shape[-1])
    gathered = lax.all_gather(weights_head, "tok", axis=1, tiled=True)
    gathered = gathered.reshape(-1, gathered.shape[-1])
    gain_rows = jnp.broadcast_to(gain[None, :], (16, gain.shape[0]))
    local_block = jnp.concatenate([tokens, gain_rows], axis=0)
    ring_size = lax.axis_size("hz")
    across_ring = lax.all_to_all(
        jnp.tile(local_block, (1, ring_size)), "hz", 1, 1, tiled=True
    )
    across_chip = lax.all_to_all(jnp.tile(across_ring, (1, 2)), "hc", 1, 1, tiled=True)
    stacked = (
        across_chip.reshape(local_block.shape[0], 2, ring_size, local_block.shape[1])
        .transpose(0, 2, 1, 3)
        .reshape(local_block.shape[0], -1)
    )
    tokens_full = stacked[:row_count]
    gain_full = stacked[row_count]
    values_wide = tokens_full.astype(jnp.float32)
    squares = jnp.sum(values_wide * values_wide, axis=1)
    factor = lax.rsqrt(squares / full_width + EPS)
    normed = (values_wide * factor[:, None] * gain_full.astype(jnp.float32)[None, :]).astype(
        jnp.bfloat16
    )
    projected = jnp.dot(normed, gathered, preferred_element_type=jnp.float32)
    projected_low = projected.astype(jnp.bfloat16)
    width_all = projected_low.shape[1]
    group_of = group_ids[:, 0]
    member = (group_of[:, None] == jnp.arange(n_tok, dtype=jnp.int32)[None, :]).astype(jnp.int32)
    local_rank = jnp.sum((jnp.cumsum(member, axis=0) - member) * member, axis=1)
    slot_index = group_of * capacity + local_rank
    counts_local = jnp.sum(member, axis=0).reshape(n_tok, 1)
    block_counts = lax.all_to_all(counts_local, "tok", 0, 0, tiled=True).reshape(n_tok)
    outgoing = (
        jnp.zeros((n_tok * capacity, width_all), jnp.bfloat16).at[slot_index].set(projected_low)
    )
    arrived = lax.all_to_all(
        outgoing.reshape(n_tok, capacity, width_all), "tok", 0, 0, tiled=True
    )
    slot_total = n_tok * capacity
    arrived = arrived.reshape(slot_total, width_all)
    live_count = (
        jnp.arange(capacity, dtype=jnp.int32)[None, :] < block_counts[:, None]
    ).astype(jnp.int32).reshape(slot_total)
    key_live = live_count > 0
    slot_rank = jnp.cumsum(live_count) - live_count
    prefix_length = page_table.shape[1] * key_pages.shape[1]
    positions = prefix_length + slot_rank
    rotated_keys = rotate(
        arrived[:, query_width : query_width + head_size].reshape(slot_total, 1, head_size),
        positions,
    )[:, 0, :]
    local_pages = page_table[0] - lax.axis_index("tok") * key_pages.shape[0]
    prefix_keys = jnp.take(key_pages[:, :, 0, :], local_pages, axis=0).reshape(
        prefix_length, head_size
    )
    prefix_values = jnp.take(value_pages[:, :, 0, :], local_pages, axis=0).reshape(
        prefix_length, head_size
    )
    attended = attend_rotating(
        arrived,
        query_width,
        positions,
        slot_rank,
        prefix_keys,
        prefix_values,
        rotated_keys,
        slot_rank,
        key_live,
    )
    returned = lax.all_to_all(
        attended.reshape(n_tok, capacity, query_width),
        "tok",
        split_axis=0,
        concat_axis=0,
        tiled=True,
    )
    return returned.reshape(n_tok * capacity, query_width)[slot_index]


def solution(mesh):
    n_tok, n_head = mesh.devices.shape
    split = jax.sharding.Mesh(mesh.devices.reshape(n_tok, n_head // 2, 2), ("tok", "hz", "hc"))
    head = ("hz", "hc")
    placed = (
        P("tok", head),
        P(head),
        P(head + ("tok",), None, None),
        P(head + ("tok",), None, None),
        P(head + ("tok",), None, None),
        P("tok", None),
        P("tok", None, head, None),
        P("tok", None, head, None),
        P("tok", None),
    )
    return jax.shard_map(
        body, mesh=split, in_specs=placed, out_specs=P("tok", head), check_vma=False
    )
```

```python
import math

import jax
import jax.numpy as jnp
from jax import lax
from jax.experimental import pallas as pl
from jax.experimental.pallas import tpu as pltpu
from jax.sharding import PartitionSpec as P

EPS = 1e-05
THETA = 10000.0


def rotate(values, positions):
    halfway = values.shape[-1] // 2
    frequency = jnp.exp(
        -math.log(THETA) * 2.0 * jnp.arange(halfway, dtype=jnp.float32) / values.shape[-1]
    )
    angles = positions.astype(jnp.float32)[:, None] * frequency[None, :]
    cosine = jnp.cos(angles)[:, None, :]
    sine_part = jnp.sin(angles)[:, None, :]
    leading = values[..., :halfway].astype(jnp.float32)
    trailing = values[..., halfway:].astype(jnp.float32)
    return jnp.concatenate(
        [leading * cosine - trailing * sine_part, trailing * cosine + leading * sine_part], axis=-1
    ).astype(jnp.bfloat16)


def attend(
    queries, query_rank, prefix_keys, prefix_values, new_keys, new_values, key_rank, key_live
):
    scaling = 1.0 / math.sqrt(queries.shape[-1])
    before = (
        jnp.einsum("bhd,pd->bhp", queries, prefix_keys, preferred_element_type=jnp.float32)
        * scaling
    )
    inside = (
        jnp.einsum("bhd,sd->bhs", queries, new_keys, preferred_element_type=jnp.float32) * scaling
    )
    allowed = key_live[None, :] & (key_rank[None, :] <= query_rank[:, None])
    inside = jnp.where(allowed[:, None, :], inside, -jnp.inf)
    highest = jnp.maximum(jnp.max(before, axis=-1), jnp.max(inside, axis=-1))
    expo_before = jnp.exp(before - highest[..., None])
    expo_inside = jnp.exp(inside - highest[..., None])
    totals = jnp.sum(expo_before, axis=-1) + jnp.sum(expo_inside, axis=-1)
    mixed = jnp.einsum(
        "bhp,pd->bhd",
        expo_before.astype(jnp.bfloat16),
        prefix_values,
        preferred_element_type=jnp.float32,
    )
    mixed = mixed + jnp.einsum(
        "bhs,sd->bhd",
        expo_inside.astype(jnp.bfloat16),
        new_values,
        preferred_element_type=jnp.float32,
    )
    return (mixed / totals[..., None]).astype(jnp.bfloat16)


def attention_kernel(q_ref, cos_ref, sin_ref, qr_ref, kp_ref, vp_ref, kn_ref, vn_ref, kr_ref, o_ref):
    size = kp_ref.shape[-1]
    heads = q_ref.shape[-1] // size
    scaling = 1.0 / math.sqrt(size)
    cosine = cos_ref[...]
    sine = sin_ref[...]
    parts = []
    for head in range(heads):
        wide = q_ref[:, head * size : (head + 1) * size].astype(jnp.float32)
        turned = pltpu.roll(wide, size // 2, 1)
        parts.append((wide * cosine + turned * sine).astype(jnp.bfloat16))
    q = jnp.concatenate(parts, axis=0)
    q_rank = jnp.concatenate([qr_ref[...]] * heads, axis=0)
    before = lax.dot_general(
        q, kp_ref[...], (((1,), (1,)), ((), ())), preferred_element_type=jnp.float32
    ) * scaling
    inside = lax.dot_general(
        q, kn_ref[...], (((1,), (1,)), ((), ())), preferred_element_type=jnp.float32
    ) * scaling
    inside = jnp.where(kr_ref[...] <= q_rank, inside, -jnp.inf)
    highest = jnp.maximum(
        jnp.max(before, axis=1, keepdims=True), jnp.max(inside, axis=1, keepdims=True)
    )
    expo_before = jnp.exp(before - highest)
    expo_inside = jnp.exp(inside - highest)
    totals = jnp.sum(expo_before, axis=1, keepdims=True) + jnp.sum(
        expo_inside, axis=1, keepdims=True
    )
    mixed = jnp.dot(
        expo_before.astype(jnp.bfloat16), vp_ref[...], preferred_element_type=jnp.float32
    ) + jnp.dot(
        expo_inside.astype(jnp.bfloat16), vn_ref[...], preferred_element_type=jnp.float32
    )
    result = (mixed / totals).astype(o_ref.dtype)
    rows = q_ref.shape[0]
    for head in range(heads):
        o_ref[:, head * size : (head + 1) * size] = result[head * rows : (head + 1) * rows]


def attend_rotating(arrived, width, positions, query_rank, prefix_keys, prefix_values, new_keys,
                    key_rank, key_live, block_slots=64):
    slots = arrived.shape[0]
    size = prefix_keys.shape[-1]
    halfway = size // 2
    frequency = jnp.exp(
        -math.log(10000.0) * 2.0 * jnp.arange(halfway, dtype=jnp.float32) / size
    )
    angles = positions.astype(jnp.float32)[:, None] * frequency[None, :]
    cosine = jnp.cos(angles)
    sine = jnp.sin(angles)
    cos_table = jnp.concatenate([cosine, cosine], axis=1)
    sin_table = jnp.concatenate([-sine, sine], axis=1)
    big = jnp.iinfo(jnp.int32).max
    k_rank = jnp.where(key_live, key_rank, big).reshape(1, -1)
    prefix_len = prefix_keys.shape[0]
    new_len = new_keys.shape[0]
    full = lambda i: (0, 0)
    by_slot = lambda i: (i, 0)
    return pl.pallas_call(
        attention_kernel,
        grid=(slots // block_slots,),
        in_specs=[
            pl.BlockSpec((block_slots, width), by_slot),
            pl.BlockSpec((block_slots, size), by_slot),
            pl.BlockSpec((block_slots, size), by_slot),
            pl.BlockSpec((block_slots, 1), by_slot),
            pl.BlockSpec((prefix_len, size), full),
            pl.BlockSpec((prefix_len, size), full),
            pl.BlockSpec((new_len, size), full),
            pl.BlockSpec((new_len, size), lambda i: (0, width // size + 1)),
            pl.BlockSpec((1, new_len), full),
        ],
        out_specs=pl.BlockSpec((block_slots, width), by_slot),
        out_shape=jax.ShapeDtypeStruct((slots, width), jnp.bfloat16),
        compiler_params=pltpu.CompilerParams(vmem_limit_bytes=48 * 1024 * 1024),
    )(arrived, cos_table, sin_table, query_rank.reshape(slots, 1), prefix_keys, prefix_values,
      new_keys, arrived, k_rank)


def row_norm(tokens, gain, full_width):
    values_wide = tokens.astype(jnp.float32)
    squares = lax.psum(jnp.sum(values_wide * values_wide, axis=1), "head")
    factor = lax.rsqrt(squares / full_width + EPS)
    return (values_wide * factor[:, None] * gain.astype(jnp.float32)[None, :]).astype(jnp.bfloat16)


def body(tokens, gain, w_query, w_key, w_value, group_ids, key_pages, value_pages, page_table):
    row_count = tokens.shape[0]
    n_tok = lax.axis_size("tok")
    n_head = lax.axis_size("head")
    head_size = key_pages.shape[-1]
    query_width = w_query.shape[2]
    group_heads = query_width // head_size
    full_width = tokens.shape[1] * n_head
    capacity = 2 * row_count // n_tok
    weights_local = jnp.concatenate([w_query, w_key, w_value], axis=2)
    head_index = lax.axis_index("head")
    pieces = [jnp.take(weights_local, head_index, axis=1)]
    for shift in range(1, n_head):
        outgoing_piece = jnp.take(weights_local, (head_index + shift) % n_head, axis=1)
        pieces.append(
            lax.ppermute(
                outgoing_piece, "head", [(j, (j + shift) % n_head) for j in range(n_head)]
            )
        )
    weights_head = jnp.take(
        jnp.stack(pieces), (head_index - jnp.arange(n_head)) % n_head, axis=0
    )
    gathered = lax.all_gather(weights_head, "tok", axis=1, tiled=True)
    gathered = gathered.reshape(-1, gathered.shape[-1])
    gain_rows = jnp.broadcast_to(gain[None, :], (16, gain.shape[0]))
    stacked = lax.all_to_all(
        jnp.tile(jnp.concatenate([tokens, gain_rows], axis=0), (1, n_head)),
        "head",
        1,
        1,
        tiled=True,
    )
    tokens_full = stacked[:row_count]
    gain_full = stacked[row_count]
    values_wide = tokens_full.astype(jnp.float32)
    squares = jnp.sum(values_wide * values_wide, axis=1)
    factor = lax.rsqrt(squares / full_width + EPS)
    normed = (values_wide * factor[:, None] * gain_full.astype(jnp.float32)[None, :]).astype(
        jnp.bfloat16
    )
    projected = jnp.dot(normed, gathered, preferred_element_type=jnp.float32)
    projected_low = projected.astype(jnp.bfloat16)
    width_all = projected_low.shape[1]
    group_of = group_ids[:, 0]
    member = (group_of[:, None] == jnp.arange(n_tok, dtype=jnp.int32)[None, :]).astype(jnp.int32)
    local_rank = jnp.sum((jnp.cumsum(member, axis=0) - member) * member, axis=1)
    slot_index = group_of * capacity + local_rank
    counts_local = jnp.sum(member, axis=0).reshape(n_tok, 1)
    block_counts = lax.all_to_all(counts_local, "tok", 0, 0, tiled=True).reshape(n_tok)
    outgoing = (
        jnp.zeros((n_tok * capacity, width_all), jnp.bfloat16).at[slot_index].set(projected_low)
    )
    arrived = lax.all_to_all(
        outgoing.reshape(n_tok, capacity, width_all), "tok", 0, 0, tiled=True
    )
    slot_total = n_tok * capacity
    arrived = arrived.reshape(slot_total, width_all)
    live_count = (
        jnp.arange(capacity, dtype=jnp.int32)[None, :] < block_counts[:, None]
    ).astype(jnp.int32).reshape(slot_total)
    key_live = live_count > 0
    slot_rank = jnp.cumsum(live_count) - live_count
    prefix_length = page_table.shape[1] * key_pages.shape[1]
    positions = prefix_length + slot_rank
    rotated_keys = rotate(
        arrived[:, query_width : query_width + head_size].reshape(slot_total, 1, head_size),
        positions,
    )[:, 0, :]
    local_pages = page_table[0] - lax.axis_index("tok") * key_pages.shape[0]
    prefix_keys = jnp.take(key_pages[:, :, 0, :], local_pages, axis=0).reshape(
        prefix_length, head_size
    )
    prefix_values = jnp.take(value_pages[:, :, 0, :], local_pages, axis=0).reshape(
        prefix_length, head_size
    )
    attended = attend_rotating(
        arrived,
        query_width,
        positions,
        slot_rank,
        prefix_keys,
        prefix_values,
        rotated_keys,
        slot_rank,
        key_live,
    )
    returned = lax.all_to_all(
        attended.reshape(n_tok, capacity, query_width),
        "tok",
        split_axis=0,
        concat_axis=0,
        tiled=True,
    )
    return returned.reshape(n_tok * capacity, query_width)[slot_index]


def solution(mesh):
    placed = (
        P("tok", "head"),
        P("head"),
        P(("head", "tok"), None, None),
        P(("head", "tok"), None, None),
        P(("head", "tok"), None, None),
        P("tok", None),
        P("tok", None, "head", None),
        P("tok", None, "head", None),
        P("tok", None),
    )
    return jax.shard_map(
        body, mesh=mesh, in_specs=placed, out_specs=P("tok", "head"), check_vma=False
    )
```

```python
import functools
import math

import jax
import jax.numpy as jnp
from jax import lax
from jax.experimental import pallas as pl
from jax.experimental.pallas import tpu as pltpu
from jax.sharding import PartitionSpec as P

EPS = 1e-05
THETA = 10000.0


def rotate(values, positions):
    halfway = values.shape[-1] // 2
    frequency = jnp.exp(
        -math.log(THETA) * 2.0 * jnp.arange(halfway, dtype=jnp.float32) / values.shape[-1]
    )
    angles = positions.astype(jnp.float32)[:, None] * frequency[None, :]
    cosine = jnp.cos(angles)[:, None, :]
    sine_part = jnp.sin(angles)[:, None, :]
    leading = values[..., :halfway].astype(jnp.float32)
    trailing = values[..., halfway:].astype(jnp.float32)
    return jnp.concatenate(
        [leading * cosine - trailing * sine_part, trailing * cosine + leading * sine_part], axis=-1
    ).astype(jnp.bfloat16)


def attend(
    queries, query_rank, prefix_keys, prefix_values, new_keys, new_values, key_rank, key_live
):
    scaling = 1.0 / math.sqrt(queries.shape[-1])
    before = (
        jnp.einsum("bhd,pd->bhp", queries, prefix_keys, preferred_element_type=jnp.float32)
        * scaling
    )
    inside = (
        jnp.einsum("bhd,sd->bhs", queries, new_keys, preferred_element_type=jnp.float32) * scaling
    )
    allowed = key_live[None, :] & (key_rank[None, :] <= query_rank[:, None])
    inside = jnp.where(allowed[:, None, :], inside, -jnp.inf)
    highest = jnp.maximum(jnp.max(before, axis=-1), jnp.max(inside, axis=-1))
    expo_before = jnp.exp(before - highest[..., None])
    expo_inside = jnp.exp(inside - highest[..., None])
    totals = jnp.sum(expo_before, axis=-1) + jnp.sum(expo_inside, axis=-1)
    mixed = jnp.einsum(
        "bhp,pd->bhd",
        expo_before.astype(jnp.bfloat16),
        prefix_values,
        preferred_element_type=jnp.float32,
    )
    mixed = mixed + jnp.einsum(
        "bhs,sd->bhd",
        expo_inside.astype(jnp.bfloat16),
        new_values,
        preferred_element_type=jnp.float32,
    )
    return (mixed / totals[..., None]).astype(jnp.bfloat16)


def attention_kernel(q_ref, cos_ref, sin_ref, qr_ref, kp_ref, vp_ref, kn_ref, vn_ref, kr_ref, o_ref):
    size = kp_ref.shape[-1]
    heads = q_ref.shape[-1] // size
    rows = q_ref.shape[0]
    scaling = 1.0 / math.sqrt(size)
    cosine = cos_ref[...]
    sine = sin_ref[...]
    parts = []
    for head in range(heads):
        wide = q_ref[:, head * size : (head + 1) * size].astype(jnp.float32)
        turned = pltpu.roll(wide, size // 2, 1)
        parts.append((wide * cosine + turned * sine).astype(jnp.bfloat16))
    q = jnp.concatenate(parts, axis=0)
    q_rank = jnp.concatenate([qr_ref[...]] * heads, axis=0)
    before = lax.dot_general(
        q, kp_ref[...], (((1,), (1,)), ((), ())), preferred_element_type=jnp.float32
    ) * scaling
    high_before = jnp.max(before, axis=1, keepdims=True)
    new_len = kn_ref.shape[0]
    chunk = min(256, new_len)
    per_chunk = max(chunk // rows, 1)
    reach = pl.program_id(0) // per_chunk

    def finish(width):
        inside = lax.dot_general(
            q, kn_ref[:width, :], (((1,), (1,)), ((), ())), preferred_element_type=jnp.float32
        ) * scaling
        inside = jnp.where(kr_ref[:, :width] <= q_rank, inside, -jnp.inf)
        highest = jnp.maximum(high_before, jnp.max(inside, axis=1, keepdims=True))
        expo_before = jnp.exp(before - highest)
        expo_inside = jnp.exp(inside - highest)
        totals = jnp.sum(expo_before, axis=1, keepdims=True) + jnp.sum(
            expo_inside, axis=1, keepdims=True
        )
        mixed = jnp.dot(
            expo_before.astype(jnp.bfloat16), vp_ref[...], preferred_element_type=jnp.float32
        ) + jnp.dot(
            expo_inside.astype(jnp.bfloat16), vn_ref[:width, :], preferred_element_type=jnp.float32
        )
        result = (mixed / totals).astype(o_ref.dtype)
        for head in range(heads):
            o_ref[:, head * size : (head + 1) * size] = result[head * rows : (head + 1) * rows]

    for part in range(new_len // chunk):
        pl.when(reach == part)(functools.partial(finish, (part + 1) * chunk))
    pl.when(reach >= new_len // chunk)(functools.partial(finish, new_len))


def attend_rotating(arrived, width, positions, query_rank, prefix_keys, prefix_values, new_keys,
                    key_rank, key_live, block_slots=64):
    slots = arrived.shape[0]
    size = prefix_keys.shape[-1]
    halfway = size // 2
    frequency = jnp.exp(
        -math.log(10000.0) * 2.0 * jnp.arange(halfway, dtype=jnp.float32) / size
    )
    angles = positions.astype(jnp.float32)[:, None] * frequency[None, :]
    cosine = jnp.cos(angles)
    sine = jnp.sin(angles)
    cos_table = jnp.concatenate([cosine, cosine], axis=1)
    sin_table = jnp.concatenate([-sine, sine], axis=1)
    big = jnp.iinfo(jnp.int32).max
    k_rank = jnp.where(key_live, key_rank, big).reshape(1, -1)
    prefix_len = prefix_keys.shape[0]
    new_len = new_keys.shape[0]
    full = lambda i: (0, 0)
    by_slot = lambda i: (i, 0)
    return pl.pallas_call(
        attention_kernel,
        grid=(slots // block_slots,),
        in_specs=[
            pl.BlockSpec((block_slots, width), by_slot),
            pl.BlockSpec((block_slots, size), by_slot),
            pl.BlockSpec((block_slots, size), by_slot),
            pl.BlockSpec((block_slots, 1), by_slot),
            pl.BlockSpec((prefix_len, size), full),
            pl.BlockSpec((prefix_len, size), full),
            pl.BlockSpec((new_len, size), full),
            pl.BlockSpec((new_len, size), lambda i: (0, width // size + 1)),
            pl.BlockSpec((1, new_len), full),
        ],
        out_specs=pl.BlockSpec((block_slots, width), by_slot),
        out_shape=jax.ShapeDtypeStruct((slots, width), jnp.bfloat16),
        compiler_params=pltpu.CompilerParams(vmem_limit_bytes=48 * 1024 * 1024),
    )(arrived, cos_table, sin_table, query_rank.reshape(slots, 1), prefix_keys, prefix_values,
      new_keys, arrived, k_rank)


def row_norm(tokens, gain, full_width):
    values_wide = tokens.astype(jnp.float32)
    squares = lax.psum(jnp.sum(values_wide * values_wide, axis=1), "head")
    factor = lax.rsqrt(squares / full_width + EPS)
    return (values_wide * factor[:, None] * gain.astype(jnp.float32)[None, :]).astype(jnp.bfloat16)


def body(tokens, gain, w_query, w_key, w_value, group_ids, key_pages, value_pages, page_table):
    row_count = tokens.shape[0]
    n_tok = lax.axis_size("tok")
    n_head = lax.axis_size("head")
    head_size = key_pages.shape[-1]
    query_width = w_query.shape[2]
    group_heads = query_width // head_size
    full_width = tokens.shape[1] * n_head
    capacity = 2 * row_count // n_tok
    weights_local = jnp.concatenate([w_query, w_key, w_value], axis=2)
    weights_head = lax.all_to_all(weights_local, "head", 1, 0, tiled=True)
    weights_head = weights_head.reshape(n_head, -1, weights_head.shape[-1])
    gathered = lax.all_gather(weights_head, "tok", axis=1, tiled=True)
    gathered = gathered.reshape(-1, gathered.shape[-1])
    gain_rows = jnp.broadcast_to(gain[None, :], (16, gain.shape[0]))
    stacked = lax.all_to_all(
        jnp.tile(jnp.concatenate([tokens, gain_rows], axis=0), (1, n_head)),
        "head",
        1,
        1,
        tiled=True,
    )
    tokens_full = stacked[:row_count]
    gain_full = stacked[row_count]
    values_wide = tokens_full.astype(jnp.float32)
    squares = jnp.sum(values_wide * values_wide, axis=1)
    factor = lax.rsqrt(squares / full_width + EPS)
    normed = (values_wide * factor[:, None] * gain_full.astype(jnp.float32)[None, :]).astype(
        jnp.bfloat16
    )
    projected = jnp.dot(normed, gathered, preferred_element_type=jnp.float32)
    projected_low = projected.astype(jnp.bfloat16)
    width_all = projected_low.shape[1]
    group_of = group_ids[:, 0]
    member = (group_of[:, None] == jnp.arange(n_tok, dtype=jnp.int32)[None, :]).astype(jnp.int32)
    local_rank = jnp.sum((jnp.cumsum(member, axis=0) - member) * member, axis=1)
    slot_index = group_of * capacity + local_rank
    counts_local = jnp.sum(member, axis=0).reshape(n_tok, 1)
    block_counts = lax.all_to_all(counts_local, "tok", 0, 0, tiled=True).reshape(n_tok)
    outgoing = (
        jnp.zeros((n_tok * capacity, width_all), jnp.bfloat16).at[slot_index].set(projected_low)
    )
    arrived = lax.all_to_all(
        outgoing.reshape(n_tok, capacity, width_all), "tok", 0, 0, tiled=True
    )
    slot_total = n_tok * capacity
    arrived = arrived.reshape(slot_total, width_all)
    live_count = (
        jnp.arange(capacity, dtype=jnp.int32)[None, :] < block_counts[:, None]
    ).astype(jnp.int32).reshape(slot_total)
    key_live = live_count > 0
    slot_rank = jnp.cumsum(live_count) - live_count
    prefix_length = page_table.shape[1] * key_pages.shape[1]
    positions = prefix_length + slot_rank
    rotated_keys = rotate(
        arrived[:, query_width : query_width + head_size].reshape(slot_total, 1, head_size),
        positions,
    )[:, 0, :]
    local_pages = page_table[0] - lax.axis_index("tok") * key_pages.shape[0]
    prefix_keys = jnp.take(key_pages[:, :, 0, :], local_pages, axis=0).reshape(
        prefix_length, head_size
    )
    prefix_values = jnp.take(value_pages[:, :, 0, :], local_pages, axis=0).reshape(
        prefix_length, head_size
    )
    attended = attend_rotating(
        arrived,
        query_width,
        positions,
        slot_rank,
        prefix_keys,
        prefix_values,
        rotated_keys,
        slot_rank,
        key_live,
    )
    returned = lax.all_to_all(
        attended.reshape(n_tok, capacity, query_width),
        "tok",
        split_axis=0,
        concat_axis=0,
        tiled=True,
    )
    return returned.reshape(n_tok * capacity, query_width)[slot_index]


def solution(mesh):
    placed = (
        P("tok", "head"),
        P("head"),
        P(("head", "tok"), None, None),
        P(("head", "tok"), None, None),
        P(("head", "tok"), None, None),
        P("tok", None),
        P("tok", None, "head", None),
        P("tok", None, "head", None),
        P("tok", None),
    )
    return jax.shard_map(
        body, mesh=mesh, in_specs=placed, out_specs=P("tok", "head"), check_vma=False
    )
```

```python
import functools
import math

import jax
import jax.numpy as jnp
from jax import lax
from jax.experimental import pallas as pl
from jax.experimental.pallas import tpu as pltpu
from jax.sharding import PartitionSpec as P

EPS = 1e-05
THETA = 10000.0


def rotate(values, positions):
    halfway = values.shape[-1] // 2
    frequency = jnp.exp(
        -math.log(THETA) * 2.0 * jnp.arange(halfway, dtype=jnp.float32) / values.shape[-1]
    )
    angles = positions.astype(jnp.float32)[:, None] * frequency[None, :]
    cosine = jnp.cos(angles)[:, None, :]
    sine_part = jnp.sin(angles)[:, None, :]
    leading = values[..., :halfway].astype(jnp.float32)
    trailing = values[..., halfway:].astype(jnp.float32)
    return jnp.concatenate(
        [leading * cosine - trailing * sine_part, trailing * cosine + leading * sine_part], axis=-1
    ).astype(jnp.bfloat16)


def attend(
    queries, query_rank, prefix_keys, prefix_values, new_keys, new_values, key_rank, key_live
):
    scaling = 1.0 / math.sqrt(queries.shape[-1])
    before = (
        jnp.einsum("bhd,pd->bhp", queries, prefix_keys, preferred_element_type=jnp.float32)
        * scaling
    )
    inside = (
        jnp.einsum("bhd,sd->bhs", queries, new_keys, preferred_element_type=jnp.float32) * scaling
    )
    allowed = key_live[None, :] & (key_rank[None, :] <= query_rank[:, None])
    inside = jnp.where(allowed[:, None, :], inside, -jnp.inf)
    highest = jnp.maximum(jnp.max(before, axis=-1), jnp.max(inside, axis=-1))
    expo_before = jnp.exp(before - highest[..., None])
    expo_inside = jnp.exp(inside - highest[..., None])
    totals = jnp.sum(expo_before, axis=-1) + jnp.sum(expo_inside, axis=-1)
    mixed = jnp.einsum(
        "bhp,pd->bhd",
        expo_before.astype(jnp.bfloat16),
        prefix_values,
        preferred_element_type=jnp.float32,
    )
    mixed = mixed + jnp.einsum(
        "bhs,sd->bhd",
        expo_inside.astype(jnp.bfloat16),
        new_values,
        preferred_element_type=jnp.float32,
    )
    return (mixed / totals[..., None]).astype(jnp.bfloat16)


def attention_kernel(q_ref, cos_ref, sin_ref, qr_ref, kp_ref, vp_ref, kn_ref, vn_ref, kr_ref, o_ref):
    size = kp_ref.shape[-1]
    heads = q_ref.shape[-1] // size
    rows = q_ref.shape[0]
    scaling = 1.0 / math.sqrt(size)
    cosine = cos_ref[...]
    sine = sin_ref[...]
    parts = []
    for head in range(heads):
        wide = q_ref[:, head * size : (head + 1) * size].astype(jnp.float32)
        turned = pltpu.roll(wide, size // 2, 1)
        parts.append((wide * cosine + turned * sine).astype(jnp.bfloat16))
    q = jnp.concatenate(parts, axis=0)
    q_rank = jnp.concatenate([qr_ref[...]] * heads, axis=0)
    before = lax.dot_general(
        q, kp_ref[...], (((1,), (1,)), ((), ())), preferred_element_type=jnp.float32
    ) * scaling
    high_before = jnp.max(before, axis=1, keepdims=True)
    new_len = kn_ref.shape[0]
    chunk = min(256, new_len)
    per_chunk = max(chunk // rows, 1)
    reach = pl.program_id(0) // per_chunk

    def finish(width):
        inside = lax.dot_general(
            q, kn_ref[:width, :], (((1,), (1,)), ((), ())), preferred_element_type=jnp.float32
        ) * scaling
        inside = jnp.where(kr_ref[:, :width] <= q_rank, inside, -jnp.inf)
        highest = jnp.maximum(high_before, jnp.max(inside, axis=1, keepdims=True))
        expo_before = jnp.exp(before - highest)
        expo_inside = jnp.exp(inside - highest)
        totals = jnp.sum(expo_before, axis=1, keepdims=True) + jnp.sum(
            expo_inside, axis=1, keepdims=True
        )
        mixed = jnp.dot(
            expo_before.astype(jnp.bfloat16), vp_ref[...], preferred_element_type=jnp.float32
        ) + jnp.dot(
            expo_inside.astype(jnp.bfloat16), vn_ref[:width, :], preferred_element_type=jnp.float32
        )
        result = (mixed / totals).astype(o_ref.dtype)
        for head in range(heads):
            o_ref[:, head * size : (head + 1) * size] = result[head * rows : (head + 1) * rows]

    for part in range(new_len // chunk):
        pl.when(reach == part)(functools.partial(finish, (part + 1) * chunk))
    pl.when(reach >= new_len // chunk)(functools.partial(finish, new_len))


def attend_rotating(arrived, width, positions, query_rank, prefix_keys, prefix_values, new_keys,
                    key_rank, key_live, block_slots=64):
    slots = arrived.shape[0]
    size = prefix_keys.shape[-1]
    halfway = size // 2
    frequency = jnp.exp(
        -math.log(10000.0) * 2.0 * jnp.arange(halfway, dtype=jnp.float32) / size
    )
    angles = positions.astype(jnp.float32)[:, None] * frequency[None, :]
    cosine = jnp.cos(angles)
    sine = jnp.sin(angles)
    cos_table = jnp.concatenate([cosine, cosine], axis=1)
    sin_table = jnp.concatenate([-sine, sine], axis=1)
    big = jnp.iinfo(jnp.int32).max
    k_rank = jnp.where(key_live, key_rank, big).reshape(1, -1)
    prefix_len = prefix_keys.shape[0]
    new_len = new_keys.shape[0]
    full = lambda i: (0, 0)
    by_slot = lambda i: (i, 0)
    return pl.pallas_call(
        attention_kernel,
        grid=(slots // block_slots,),
        in_specs=[
            pl.BlockSpec((block_slots, width), by_slot),
            pl.BlockSpec((block_slots, size), by_slot),
            pl.BlockSpec((block_slots, size), by_slot),
            pl.BlockSpec((block_slots, 1), by_slot),
            pl.BlockSpec((prefix_len, size), full),
            pl.BlockSpec((prefix_len, size), full),
            pl.BlockSpec((new_len, size), full),
            pl.BlockSpec((new_len, size), lambda i: (0, width // size + 1)),
            pl.BlockSpec((1, new_len), full),
        ],
        out_specs=pl.BlockSpec((block_slots, width), by_slot),
        out_shape=jax.ShapeDtypeStruct((slots, width), jnp.bfloat16),
        compiler_params=pltpu.CompilerParams(vmem_limit_bytes=48 * 1024 * 1024),
    )(arrived, cos_table, sin_table, query_rank.reshape(slots, 1), prefix_keys, prefix_values,
      new_keys, arrived, k_rank)


def row_norm(tokens, gain, full_width):
    values_wide = tokens.astype(jnp.float32)
    squares = lax.psum(jnp.sum(values_wide * values_wide, axis=1), "head")
    factor = lax.rsqrt(squares / full_width + EPS)
    return (values_wide * factor[:, None] * gain.astype(jnp.float32)[None, :]).astype(jnp.bfloat16)


def body(tokens, gain, w_query, w_key, w_value, group_ids, key_pages, value_pages, page_table):
    row_count = tokens.shape[0]
    n_tok = lax.axis_size("tok")
    n_head = lax.axis_size("head")
    head_size = key_pages.shape[-1]
    query_width = w_query.shape[2]
    group_heads = query_width // head_size
    full_width = tokens.shape[1] * n_head
    capacity = 2 * row_count // n_tok
    weights_local = jnp.concatenate([w_query, w_key, w_value], axis=2)
    weights_head = lax.all_to_all(weights_local, "head", 1, 0, tiled=True)
    weights_head = weights_head.reshape(n_head, -1, weights_head.shape[-1])
    group_of = group_ids[:, 0]
    member = (group_of[:, None] == jnp.arange(n_tok, dtype=jnp.int32)[None, :]).astype(jnp.int32)
    count_slab = jnp.zeros((1,) + weights_head.shape[1:], jnp.bfloat16)
    count_slab = count_slab.at[0, 0, :n_tok].set(jnp.sum(member, axis=0).astype(jnp.bfloat16))
    gathered_all = lax.all_gather(
        jnp.concatenate([weights_head, count_slab], axis=0), "tok", axis=1, tiled=True
    )
    block_counts = gathered_all[n_head, :: weights_head.shape[1], lax.axis_index("tok")]
    block_counts = block_counts.astype(jnp.int32)
    gathered = gathered_all[:n_head].reshape(-1, gathered_all.shape[-1])
    gain_rows = jnp.broadcast_to(gain[None, :], (16, gain.shape[0]))
    stacked = lax.all_to_all(
        jnp.tile(jnp.concatenate([tokens, gain_rows], axis=0), (1, n_head)),
        "head",
        1,
        1,
        tiled=True,
    )
    tokens_full = stacked[:row_count]
    gain_full = stacked[row_count]
    values_wide = tokens_full.astype(jnp.float32)
    squares = jnp.sum(values_wide * values_wide, axis=1)
    factor = lax.rsqrt(squares / full_width + EPS)
    normed = (values_wide * factor[:, None] * gain_full.astype(jnp.float32)[None, :]).astype(
        jnp.bfloat16
    )
    projected = jnp.dot(normed, gathered, preferred_element_type=jnp.float32)
    projected_low = projected.astype(jnp.bfloat16)
    width_all = projected_low.shape[1]
    local_rank = jnp.sum((jnp.cumsum(member, axis=0) - member) * member, axis=1)
    slot_index = group_of * capacity + local_rank
    outgoing = (
        jnp.zeros((n_tok * capacity, width_all), jnp.bfloat16).at[slot_index].set(projected_low)
    )
    arrived = lax.all_to_all(
        outgoing.reshape(n_tok, capacity, width_all), "tok", 0, 0, tiled=True
    )
    slot_total = n_tok * capacity
    arrived = arrived.reshape(slot_total, width_all)
    live_count = (
        jnp.arange(capacity, dtype=jnp.int32)[None, :] < block_counts[:, None]
    ).astype(jnp.int32).reshape(slot_total)
    key_live = live_count > 0
    slot_rank = jnp.cumsum(live_count) - live_count
    prefix_length = page_table.shape[1] * key_pages.shape[1]
    positions = prefix_length + slot_rank
    rotated_keys = rotate(
        arrived[:, query_width : query_width + head_size].reshape(slot_total, 1, head_size),
        positions,
    )[:, 0, :]
    local_pages = page_table[0] - lax.axis_index("tok") * key_pages.shape[0]
    prefix_keys = jnp.take(key_pages[:, :, 0, :], local_pages, axis=0).reshape(
        prefix_length, head_size
    )
    prefix_values = jnp.take(value_pages[:, :, 0, :], local_pages, axis=0).reshape(
        prefix_length, head_size
    )
    attended = attend_rotating(
        arrived,
        query_width,
        positions,
        slot_rank,
        prefix_keys,
        prefix_values,
        rotated_keys,
        slot_rank,
        key_live,
    )
    returned = lax.all_to_all(
        attended.reshape(n_tok, capacity, query_width),
        "tok",
        split_axis=0,
        concat_axis=0,
        tiled=True,
    )
    return returned.reshape(n_tok * capacity, query_width)[slot_index]


def solution(mesh):
    placed = (
        P("tok", "head"),
        P("head"),
        P(("head", "tok"), None, None),
        P(("head", "tok"), None, None),
        P(("head", "tok"), None, None),
        P("tok", None),
        P("tok", None, "head", None),
        P("tok", None, "head", None),
        P("tok", None),
    )
    return jax.shard_map(
        body, mesh=mesh, in_specs=placed, out_specs=P("tok", "head"), check_vma=False
    )
```

```python
import functools
import math

import jax
import jax.numpy as jnp
from jax import lax
from jax.experimental import pallas as pl
from jax.experimental.pallas import tpu as pltpu
from jax.sharding import PartitionSpec as P

EPS = 1e-05
THETA = 10000.0


def rotate(values, positions):
    halfway = values.shape[-1] // 2
    frequency = jnp.exp(
        -math.log(THETA) * 2.0 * jnp.arange(halfway, dtype=jnp.float32) / values.shape[-1]
    )
    angles = positions.astype(jnp.float32)[:, None] * frequency[None, :]
    cosine = jnp.cos(angles)[:, None, :]
    sine_part = jnp.sin(angles)[:, None, :]
    leading = values[..., :halfway].astype(jnp.float32)
    trailing = values[..., halfway:].astype(jnp.float32)
    return jnp.concatenate(
        [leading * cosine - trailing * sine_part, trailing * cosine + leading * sine_part], axis=-1
    ).astype(jnp.bfloat16)


def attend(
    queries, query_rank, prefix_keys, prefix_values, new_keys, new_values, key_rank, key_live
):
    scaling = 1.0 / math.sqrt(queries.shape[-1])
    before = (
        jnp.einsum("bhd,pd->bhp", queries, prefix_keys, preferred_element_type=jnp.float32)
        * scaling
    )
    inside = (
        jnp.einsum("bhd,sd->bhs", queries, new_keys, preferred_element_type=jnp.float32) * scaling
    )
    allowed = key_live[None, :] & (key_rank[None, :] <= query_rank[:, None])
    inside = jnp.where(allowed[:, None, :], inside, -jnp.inf)
    highest = jnp.maximum(jnp.max(before, axis=-1), jnp.max(inside, axis=-1))
    expo_before = jnp.exp(before - highest[..., None])
    expo_inside = jnp.exp(inside - highest[..., None])
    totals = jnp.sum(expo_before, axis=-1) + jnp.sum(expo_inside, axis=-1)
    mixed = jnp.einsum(
        "bhp,pd->bhd",
        expo_before.astype(jnp.bfloat16),
        prefix_values,
        preferred_element_type=jnp.float32,
    )
    mixed = mixed + jnp.einsum(
        "bhs,sd->bhd",
        expo_inside.astype(jnp.bfloat16),
        new_values,
        preferred_element_type=jnp.float32,
    )
    return (mixed / totals[..., None]).astype(jnp.bfloat16)


def attention_kernel(q_ref, cos_ref, sin_ref, qr_ref, kp_ref, vp_ref, kn_ref, vn_ref, kr_ref, o_ref):
    size = kp_ref.shape[-1]
    heads = q_ref.shape[-1] // size
    rows = q_ref.shape[0]
    scaling = 1.0 / math.sqrt(size)
    cosine = cos_ref[...]
    sine = sin_ref[...]
    parts = []
    for head in range(heads):
        wide = q_ref[:, head * size : (head + 1) * size].astype(jnp.float32)
        turned = pltpu.roll(wide, size // 2, 1)
        parts.append((wide * cosine + turned * sine).astype(jnp.bfloat16))
    q = jnp.concatenate(parts, axis=0)
    q_rank = jnp.concatenate([qr_ref[...]] * heads, axis=0)
    before = lax.dot_general(
        q, kp_ref[...], (((1,), (1,)), ((), ())), preferred_element_type=jnp.float32
    ) * scaling
    high_before = jnp.max(before, axis=1, keepdims=True)
    new_len = kn_ref.shape[0]
    chunk = min(256, new_len)
    per_chunk = max(chunk // rows, 1)
    reach = pl.program_id(0) // per_chunk

    def finish(width):
        inside = lax.dot_general(
            q, kn_ref[:width, :], (((1,), (1,)), ((), ())), preferred_element_type=jnp.float32
        ) * scaling
        inside = jnp.where(kr_ref[:, :width] <= q_rank, inside, -jnp.inf)
        highest = jnp.maximum(high_before, jnp.max(inside, axis=1, keepdims=True))
        expo_before = jnp.exp(before - highest)
        expo_inside = jnp.exp(inside - highest)
        totals = jnp.sum(expo_before, axis=1, keepdims=True) + jnp.sum(
            expo_inside, axis=1, keepdims=True
        )
        mixed = jnp.dot(
            expo_before.astype(jnp.bfloat16), vp_ref[...], preferred_element_type=jnp.float32
        ) + jnp.dot(
            expo_inside.astype(jnp.bfloat16), vn_ref[:width, :], preferred_element_type=jnp.float32
        )
        result = (mixed / totals).astype(o_ref.dtype)
        for head in range(heads):
            o_ref[:, head * size : (head + 1) * size] = result[head * rows : (head + 1) * rows]

    for part in range(new_len // chunk):
        pl.when(reach == part)(functools.partial(finish, (part + 1) * chunk))
    pl.when(reach >= new_len // chunk)(functools.partial(finish, new_len))


def attend_rotating(arrived, width, positions, query_rank, prefix_keys, prefix_values, new_keys,
                    key_rank, key_live, block_slots=64):
    slots = arrived.shape[0]
    size = prefix_keys.shape[-1]
    halfway = size // 2
    frequency = jnp.exp(
        -math.log(10000.0) * 2.0 * jnp.arange(halfway, dtype=jnp.float32) / size
    )
    angles = positions.astype(jnp.float32)[:, None] * frequency[None, :]
    cosine = jnp.cos(angles)
    sine = jnp.sin(angles)
    cos_table = jnp.concatenate([cosine, cosine], axis=1)
    sin_table = jnp.concatenate([-sine, sine], axis=1)
    big = jnp.iinfo(jnp.int32).max
    k_rank = jnp.where(key_live, key_rank, big).reshape(1, -1)
    prefix_len = prefix_keys.shape[0]
    new_len = new_keys.shape[0]
    full = lambda i: (0, 0)
    by_slot = lambda i: (i, 0)
    return pl.pallas_call(
        attention_kernel,
        grid=(slots // block_slots,),
        in_specs=[
            pl.BlockSpec((block_slots, width), by_slot),
            pl.BlockSpec((block_slots, size), by_slot),
            pl.BlockSpec((block_slots, size), by_slot),
            pl.BlockSpec((block_slots, 1), by_slot),
            pl.BlockSpec((prefix_len, size), full),
            pl.BlockSpec((prefix_len, size), full),
            pl.BlockSpec((new_len, size), full),
            pl.BlockSpec((new_len, size), lambda i: (0, width // size + 1)),
            pl.BlockSpec((1, new_len), full),
        ],
        out_specs=pl.BlockSpec((block_slots, width), by_slot),
        out_shape=jax.ShapeDtypeStruct((slots, width), jnp.bfloat16),
        compiler_params=pltpu.CompilerParams(vmem_limit_bytes=48 * 1024 * 1024),
    )(arrived, cos_table, sin_table, query_rank.reshape(slots, 1), prefix_keys, prefix_values,
      new_keys, arrived, k_rank)


def row_norm(tokens, gain, full_width):
    values_wide = tokens.astype(jnp.float32)
    squares = lax.psum(jnp.sum(values_wide * values_wide, axis=1), "head")
    factor = lax.rsqrt(squares / full_width + EPS)
    return (values_wide * factor[:, None] * gain.astype(jnp.float32)[None, :]).astype(jnp.bfloat16)


def body(tokens, gain, w_query, w_key, w_value, group_ids, key_pages, value_pages, page_table):
    row_count = tokens.shape[0]
    n_tok = lax.axis_size("tok")
    n_head = lax.axis_size("head")
    head_size = key_pages.shape[-1]
    query_width = w_query.shape[2]
    group_heads = query_width // head_size
    full_width = tokens.shape[1] * n_head
    capacity = 2 * row_count // n_tok
    weights_local = jnp.concatenate([w_query, w_key, w_value], axis=2)
    weights_head = lax.all_to_all(weights_local, "head", 1, 0, tiled=True)
    weights_head = weights_head.reshape(n_head, -1, weights_head.shape[-1])
    group_of = group_ids[:, 0]
    member = (group_of[:, None] == jnp.arange(n_tok, dtype=jnp.int32)[None, :]).astype(jnp.int32)
    count_slab = jnp.zeros((1,) + weights_head.shape[1:], jnp.bfloat16)
    count_slab = count_slab.at[0, 0, :n_tok].set(jnp.sum(member, axis=0).astype(jnp.bfloat16))
    gathered_all = lax.all_gather(
        jnp.concatenate([weights_head, count_slab], axis=0), "tok", axis=1, tiled=True
    )
    block_counts = gathered_all[n_head, :: weights_head.shape[1], lax.axis_index("tok")]
    block_counts = block_counts.astype(jnp.int32)
    gathered = gathered_all[:n_head].reshape(-1, gathered_all.shape[-1])
    gain_rows = jnp.broadcast_to(gain[None, :], (16, gain.shape[0]))
    stacked = lax.all_to_all(
        jnp.tile(jnp.concatenate([tokens, gain_rows], axis=0), (1, n_head)),
        "head",
        1,
        1,
        tiled=True,
    )
    tokens_full = stacked[:row_count]
    gain_full = stacked[row_count]
    values_wide = tokens_full.astype(jnp.float32)
    squares = jnp.sum(values_wide * values_wide, axis=1)
    factor = lax.rsqrt(squares / full_width + EPS)
    normed = (values_wide * factor[:, None] * gain_full.astype(jnp.float32)[None, :]).astype(
        jnp.bfloat16
    )
    projected = jnp.dot(normed, gathered, preferred_element_type=jnp.float32)
    projected_low = projected.astype(jnp.bfloat16)
    width_all = projected_low.shape[1]
    local_rank = jnp.sum((jnp.cumsum(member, axis=0) - member) * member, axis=1)
    slot_index = group_of * capacity + local_rank
    source_row = (
        jnp.zeros((n_tok * capacity,), jnp.int32)
        .at[slot_index]
        .set(jnp.arange(row_count, dtype=jnp.int32))
    )
    outgoing = jnp.take(projected_low, source_row, axis=0)
    arrived = lax.all_to_all(
        outgoing.reshape(n_tok, capacity, width_all), "tok", 0, 0, tiled=True
    )
    slot_total = n_tok * capacity
    arrived = arrived.reshape(slot_total, width_all)
    live_count = (
        jnp.arange(capacity, dtype=jnp.int32)[None, :] < block_counts[:, None]
    ).astype(jnp.int32).reshape(slot_total)
    key_live = live_count > 0
    slot_rank = jnp.cumsum(live_count) - live_count
    prefix_length = page_table.shape[1] * key_pages.shape[1]
    positions = prefix_length + slot_rank
    rotated_keys = rotate(
        arrived[:, query_width : query_width + head_size].reshape(slot_total, 1, head_size),
        positions,
    )[:, 0, :]
    local_pages = page_table[0] - lax.axis_index("tok") * key_pages.shape[0]
    prefix_keys = jnp.take(key_pages[:, :, 0, :], local_pages, axis=0).reshape(
        prefix_length, head_size
    )
    prefix_values = jnp.take(value_pages[:, :, 0, :], local_pages, axis=0).reshape(
        prefix_length, head_size
    )
    attended = attend_rotating(
        arrived,
        query_width,
        positions,
        slot_rank,
        prefix_keys,
        prefix_values,
        rotated_keys,
        slot_rank,
        key_live,
    )
    returned = lax.all_to_all(
        attended.reshape(n_tok, capacity, query_width),
        "tok",
        split_axis=0,
        concat_axis=0,
        tiled=True,
    )
    return returned.reshape(n_tok * capacity, query_width)[slot_index]


def solution(mesh):
    placed = (
        P("tok", "head"),
        P("head"),
        P(("head", "tok"), None, None),
        P(("head", "tok"), None, None),
        P(("head", "tok"), None, None),
        P("tok", None),
        P("tok", None, "head", None),
        P("tok", None, "head", None),
        P("tok", None),
    )
    return jax.shard_map(
        body, mesh=mesh, in_specs=placed, out_specs=P("tok", "head"), check_vma=False
    )
```
